32 devices in a mesh: comp: 2 (over y), gx: 4 (over x, core), gy: 4 (over z).
Axes of the slice: x: 2, y: 2, z: 4, core: 2. Of those that a mesh axis runs over, the one named last changes fastest.
Arguments:
- state: float32 [2, 16, 512, 512], P('comp', None, 'gx', 'gy'), may hold values from -6 to 6
- velocity: bfloat16 [2, 2, 16, 512, 512], P('comp', None, None, 'gx', 'gy'), may hold values from -0.5 to 0.5
- diffusivity: float32 [2, 16], P('comp'), may hold values from 0.02 to 0.2
- export_proj: float32 [2, 8, 16], P('comp'), may hold values from -1.5 to 1.5
- import_proj: float32 [2, 16, 8], P('comp'), may hold values from -2 to 2
- intersection_weights: bfloat16 [2, 512, 4, 4, 128, 128], P('comp', 'gx', 'gy'), may hold values from -0.25 to 0.25
- recv_slots: int32 [2, 512, 4, 4], P('comp', 'gx', 'gy'), may hold values from 0 to 1023, as said below
- send_slots: int32 [2, 4, 4, 16, 64], P(None, 'gx', 'gy'), may hold values from 0 to 127, as said below
- land: int32 [512, 4], P('gx', 'gy'), may hold values 0 or 1
Outputs:
- new_state: float32 [2, 16, 512, 512], P('comp', None, 'gx', 'gy')
- imported: bfloat16 [2, 512, 8, 512], P('comp', 'gx', None, 'gy')
The draws below stay inside these ranges and needn't reach their ends.
Inputs may be any that keep to these rules, and one draw needn't show every extreme that they name: `recv_slots`: entry p names the place, source device times 64 plus place, in the buffer from the other component; each destination device reads each place at most once; at most 64 of one destination device's tiles' references come from one source device, and for every destination device exactly 64 come from one source device. Source devices are numbered row-major over gx and gy. `send_slots`: entry [c, a, b, d, q] is the local block row that source device (a, b) of component c puts into place q of its buffer for destination device d of the other component; places that no destination reads hold 0.
All inputs are finite; a program needn't handle non-finite values. No bound on the sum of `land` on one device may be relied on, other than what follows from the above.
Results may differ from the reference program's by a relative error of at most 0.0049.
Values may be sent and summed in bfloat16 or wider, within the bound.
No kernel may reach another device: no remote copies, remote signals or barrier semaphores. Data moves between devices by JAX's collectives and lax.ppermute only.
A program may use at most 128 MiB of HBM per device.

```python
import math
import jax
import jax.numpy as jnp
from jax import lax

LEV = 16
CX = 128
TILE = 128
FLD = 8
K = 4
STEPS = 2
ROWS = 512
COLS = 512
GROUP = 16
CAP = 64
N_GX = 4
N_GY = 4


def intersection_tables(key):
    base_key = jax.random.fold_in(key, 7)
    slots_total = GROUP * CAP
    ref_count = CX * K
    sub_keys = jax.random.split(base_key, 2 * GROUP)

    def draw_one(sub_key):
        key_full, key_perm, key_refs, key_tiles = jax.random.split(sub_key, 4)
        full_source = jax.random.randint(key_full, (), 0, GROUP)
        shuffled = jax.random.permutation(key_perm, slots_total).astype(jnp.int32)
        rank_of = jnp.argsort(shuffled).astype(jnp.int32)
        places = jnp.arange(slots_total, dtype=jnp.int32)
        priority = jnp.where(places // CAP == full_source, places - slots_total, rank_of)
        ordered = jnp.argsort(priority).astype(jnp.int32)
        used_slots = ordered[:ref_count]
        picked = used_slots[jax.random.permutation(key_refs, ref_count)]
        used_marks = jnp.zeros((slots_total,), jnp.int32).at[used_slots].set(1)
        tile_rows = jax.random.randint(key_tiles, (slots_total,), 0, CX) * used_marks
        return (picked, tile_rows)
    picked, tile_rows = jax.vmap(draw_one)(sub_keys)
    recv_table = picked.reshape(2, N_GX, N_GY, CX, K).transpose(0, 1, 3, 2, 4).reshape(2, ROWS, N_GY, K)
    send_table = tile_rows.reshape(2, GROUP, GROUP, CAP).transpose(0, 2, 1, 3)[::-1].reshape(2, N_GX, N_GY, GROUP, CAP)
    return (recv_table.astype(jnp.int32), send_table.astype(jnp.int32))


def draw_recv_slots(key, part):
    return intersection_tables(key)[0]


def draw_send_slots(key, part):
    return intersection_tables(key)[1]


def plant(result, key, least, high):
    longest = result.shape.index(max(result.shape))
    spots = []
    for shift in (0, 1):
        where = [jax.random.randint(jax.random.fold_in(key, axis), (), 0, length) for axis, length in enumerate(result.shape)]
        where[longest] = (where[longest] + shift) % result.shape[longest]
        spots.append(tuple(where))
    return result.at[spots[0]].set(least).at[spots[1]].set(high)


def steps_of(key, shape, cuts, smallest, high):
    gain = 1.0
    for position, parts in cuts:
        draws = jax.random.uniform(jax.random.fold_in(jax.random.fold_in(key, 6), position), (parts,), jnp.float32, smallest / len(cuts), high / len(cuts))
        gain = gain * jnp.repeat(jnp.exp(draws), shape[position] // parts).reshape((-1,) + (1,) * (len(shape) - 1 - position))
    return gain


def gaussian(key, dims, width, reach, shards=(), held_as=jnp.bfloat16):
    array = jax.random.normal(key, dims, jnp.float32) * width
    if len(shards) > 0:
        array = steps_of(key, dims, shards, -0.22, 0.18) * array
    return jnp.clip(array, min=-reach, max=reach).astype(held_as)


def setup_inputs(seed: int = 0) -> dict:
    key_list = jax.random.split(jax.random.key(seed), 10)
    return {
        "state": gaussian(key_list[0], (2, LEV, ROWS, COLS), 1.0, 6.0, ((0, 2), (2, 4), (3, 4)), jnp.float32),
        "velocity": jnp.clip(jax.random.uniform(key_list[1], (2, 2, LEV, ROWS, COLS), jnp.float32, -0.5, 0.5) * steps_of(key_list[1], (2, 2, LEV, ROWS, COLS), ((0, 2), (3, 4), (4, 4)), -0.4, 0.0), -0.5, 0.5).astype(jnp.bfloat16),
        "diffusivity": jnp.clip(jnp.exp(math.log(0.2) - 2.3025851 * jax.random.uniform(key_list[2], (2, LEV), jnp.float32) ** steps_of(key_list[2], (2, LEV), ((0, 2),), -0.2, 0.2)), 0.02, 0.2),
        "export_proj": gaussian(key_list[3], (2, FLD, LEV), LEV ** -0.5, 1.5, ((0, 2),), jnp.float32),
        "import_proj": gaussian(key_list[4], (2, LEV, FLD), FLD ** -0.5, 2.0, ((0, 2),), jnp.float32),
        "intersection_weights": gaussian(key_list[5], (2, ROWS, N_GY, K, TILE, TILE), (K * TILE) ** -0.5, 0.25, ((0, 2), (1, 4), (2, 4))),
        "recv_slots": draw_recv_slots(jax.random.fold_in(key_list[9], 71), 0),
        "send_slots": draw_send_slots(jax.random.fold_in(key_list[9], 71), 0),
        "land": plant((jax.random.randint(key_list[8], (ROWS, N_GY), 0, 10) < 7).astype(jnp.int32), jax.random.fold_in(key_list[8], 1), 0, 1),
    }


def advance(tracer, speeds, coeffs, wet_mask):
    padded = jnp.pad(tracer, ((0, 0), (1, 1), (1, 1)))
    row_down = padded[:, 2:, 1:-1]
    row_up = padded[:, :-2, 1:-1]
    col_right = padded[:, 1:-1, 2:]
    col_left = padded[:, 1:-1, :-2]
    spread = row_down + row_up + col_right + col_left - 4.0 * tracer
    carried = 0.5 * (speeds[0].astype(jnp.float32) * (row_down - row_up) + speeds[1].astype(jnp.float32) * (col_right - col_left))
    return tracer + wet_mask * (coeffs[:, None, None] * spread - carried)


def reference(state, velocity, diffusivity, export_proj, import_proj, intersection_weights, recv_slots, send_slots, land):
    highest = lax.Precision.HIGHEST
    wet_ocean = jnp.repeat(land.astype(jnp.float32), TILE, axis=1)
    wet_cells = jnp.stack([jnp.ones_like(wet_ocean), wet_ocean])
    wet_tiles = jnp.stack([jnp.ones(land.shape, jnp.float32), land.astype(jnp.float32)])
    exported = (jnp.einsum("cfl,clxy->cfxy", export_proj, state, precision=highest) * wet_cells[:, None]).astype(jnp.bfloat16)
    tile_set = exported.reshape(2, FLD, N_GX, CX, N_GY, TILE).transpose(0, 2, 4, 3, 1, 5).reshape(2, GROUP * CX, FLD, TILE)
    send_flat = send_slots.reshape(2, GROUP, GROUP, CAP)
    dest_dev = (jnp.arange(ROWS, dtype=jnp.int32)[:, None] // CX) * N_GY + jnp.arange(N_GY, dtype=jnp.int32)[None, :]
    source_dev = (recv_slots // CAP).astype(jnp.int32)
    source_place = (recv_slots % CAP).astype(jnp.int32)
    source_comp = (1 - jnp.arange(2, dtype=jnp.int32))[:, None, None, None]
    local_row = send_flat[source_comp, source_dev, dest_dev[None, :, :, None], source_place]
    gathered = tile_set[source_comp, (source_dev * CX + local_row).astype(jnp.int32)]

    def one_row(pair):
        pieces, weights = pair
        return jnp.einsum("bkfm,bkom->bfo", pieces.astype(jnp.float32), weights.astype(jnp.float32), precision=highest)

    summed = lax.map(one_row, (gathered.reshape(2 * ROWS, N_GY, K, FLD, TILE), intersection_weights.reshape(2 * ROWS, N_GY, K, TILE, TILE)))
    summed = summed.reshape(2, ROWS, N_GY, FLD, TILE) * wet_tiles[:, :, :, None, None]
    imported = summed.astype(jnp.bfloat16).transpose(0, 1, 3, 2, 4).reshape(2, ROWS, FLD, COLS)
    results = []
    for section in range(2):
        tracer = state[section]
        for repeat in range(STEPS):
            tracer = advance(tracer, velocity[section], diffusivity[section], wet_cells[section])
        forcing = jnp.einsum("lf,xfy->lxy", import_proj[section], imported[section].astype(jnp.float32), precision=highest)
        results.append(tracer + wet_cells[section] * forcing)
    return jnp.stack(results), imported
```

```python
import jax
import jax.numpy as jnp
from jax import lax
from jax.sharding import PartitionSpec as P

STEPS = 2


def padded_2(cells, sides, width):
    for axis, dim in sides:
        count = lax.axis_size(axis)
        ends = count - 1
        head = lax.slice_in_dim(cells, 0, width, axis=dim)
        tail = lax.slice_in_dim(cells, cells.shape[dim] - width, cells.shape[dim], axis=dim)
        cells = jnp.concatenate(
            [
                lax.ppermute(tail, axis, [(i, (i + 1) % count) for i in range(ends)]),
                cells,
                lax.ppermute(head, axis, [((i + 1) % count, i) for i in range(ends)]),
            ],
            axis=dim,
        )
    return cells


def advance(tracer, speeds, coeffs, wet_mask):
    padded = padded_2(tracer.astype(jnp.bfloat16), (("gx", 1), ("gy", 2)), 1).astype(tracer.dtype)
    row_down = padded[:, 2:, 1:-1]
    row_up = padded[:, :-2, 1:-1]
    col_right = padded[:, 1:-1, 2:]
    col_left = padded[:, 1:-1, :-2]
    spread = row_down + row_up + col_right + col_left - 4.0 * tracer
    carried = 0.5 * (
        speeds[0].astype(jnp.float32) * (row_down - row_up)
        + speeds[1].astype(jnp.float32) * (col_right - col_left)
    )
    return tracer + wet_mask * (coeffs[:, None, None] * spread - carried)


def exchange(exports, own_table, recv):
    n_gx = lax.axis_size("gx")
    n_gy = lax.axis_size("gy")
    group = n_gx * n_gy
    cap = own_table.shape[1]
    section = lax.axis_index("comp")
    a = lax.axis_index("gx")
    b = lax.axis_index("gy")
    shifts = jnp.arange(group, dtype=jnp.int32)
    da = shifts // n_gy
    db = shifts % n_gy
    dest = ((a + da) % n_gx) * n_gy + (b + db) % n_gy
    packed = exports[own_table[dest]]
    axes = ("comp", "gx", "gy")
    pieces = []
    for k in range(group):
        sa, sb = k // n_gy, k % n_gy
        perm = []
        for c in range(2):
            for i in range(n_gx):
                for j in range(n_gy):
                    src = (c * n_gx + i) * n_gy + j
                    dst = ((1 - c) * n_gx + (i + sa) % n_gx) * n_gy + (j + sb) % n_gy
                    perm.append((src, dst))
        pieces.append(lax.ppermute(packed[k], axes, perm))
    arrived = jnp.stack(pieces).reshape(group * cap, exports.shape[1], exports.shape[2])
    source = recv // cap
    place = recv % cap
    k_of = ((a - source // n_gy) % n_gx) * n_gy + (b - source % n_gy) % n_gy
    return arrived[k_of * cap + place]


def per_device(
    state,
    velocity,
    diffusivity,
    export_proj,
    import_proj,
    intersection_weights,
    recv_slots,
    send_slots,
    land,
):
    highest = lax.Precision.HIGHEST
    section = lax.axis_index("comp")
    tracer = state[0]
    wet_tile = jnp.where(section == 0, jnp.ones(land.shape, jnp.float32), land.astype(jnp.float32))
    exports = (
        jnp.einsum("fl,lxy->xfy", export_proj[0], tracer, precision=highest) * wet_tile[:, :, None]
    ).astype(jnp.bfloat16)
    tables = send_slots[:, 0, 0]
    own_table = lax.dynamic_index_in_dim(tables, section, 0, keepdims=False)
    sources = exchange(exports, own_table, recv_slots[0, :, 0, :])
    summed = lax.dot_general(
        sources,
        intersection_weights[0, :, 0],
        (((1, 3), (1, 3)), ((0,), (0,))),
        preferred_element_type=jnp.float32,
    )
    imported = (summed * wet_tile[:, :, None]).astype(jnp.bfloat16)
    wet_cells = wet_tile[None]
    for repeat in range(STEPS):
        tracer = advance(tracer, velocity[0], diffusivity[0], wet_cells)
    forcing = jnp.einsum(
        "lf,xfy->lxy", import_proj[0], imported.astype(jnp.float32), precision=highest
    )
    return ((tracer + wet_cells * forcing)[None], imported[None])


def solution(mesh):
    return jax.shard_map(
        per_device,
        mesh=mesh,
        in_specs=(
            P("comp", None, "gx", "gy"),
            P("comp", None, None, "gx", "gy"),
            P("comp", None),
            P("comp", None, None),
            P("comp", None, None),
            P("comp", "gx", "gy", None, None, None),
            P("comp", "gx", "gy", None),
            P(None, "gx", "gy", None, None),
            P("gx", "gy"),
        ),
        out_specs=(P("comp", None, "gx", "gy"), P("comp", "gx", None, "gy")),
        check_vma=False,
    )
```

```python
import jax
import jax.numpy as jnp
from jax import lax
from jax.experimental import pallas as pl
from jax.experimental.pallas import tpu as pltpu
from jax.sharding import PartitionSpec as P

STEPS = 2


def padded_2(cells, sides, width):
    for axis, dim in sides:
        count = lax.axis_size(axis)
        ends = count - 1
        head = lax.slice_in_dim(cells, 0, width, axis=dim)
        tail = lax.slice_in_dim(cells, cells.shape[dim] - width, cells.shape[dim], axis=dim)
        cells = jnp.concatenate(
            [
                lax.ppermute(tail, axis, [(i, (i + 1) % count) for i in range(ends)]),
                cells,
                lax.ppermute(head, axis, [((i + 1) % count, i) for i in range(ends)]),
            ],
            axis=dim,
        )
    return cells


def advance(tracer, speeds, coeffs, wet_mask):
    padded = padded_2(tracer.astype(jnp.bfloat16), (("gx", 1), ("gy", 2)), 1).astype(tracer.dtype)
    row_down = padded[:, 2:, 1:-1]
    row_up = padded[:, :-2, 1:-1]
    col_right = padded[:, 1:-1, 2:]
    col_left = padded[:, 1:-1, :-2]
    spread = row_down + row_up + col_right + col_left - 4.0 * tracer
    carried = 0.5 * (
        speeds[0].astype(jnp.float32) * (row_down - row_up)
        + speeds[1].astype(jnp.float32) * (col_right - col_left)
    )
    return tracer + wet_mask * (coeffs[:, None, None] * spread - carried)


def exchange(exports, own_table):
    n_gx = lax.axis_size("gx")
    n_gy = lax.axis_size("gy")
    group = n_gx * n_gy
    a = lax.axis_index("gx")
    b = lax.axis_index("gy")
    shifts = jnp.arange(group, dtype=jnp.int32)
    dest = ((a + shifts // n_gy) % n_gx) * n_gy + (b + shifts % n_gy) % n_gy
    packed = exports[own_table[dest]]
    axes = ("comp", "gx", "gy")
    pieces = []
    for k in range(group):
        sa, sb = k // n_gy, k % n_gy
        perm = []
        for c in range(2):
            for i in range(n_gx):
                for j in range(n_gy):
                    src = (c * n_gx + i) * n_gy + j
                    dst = ((1 - c) * n_gx + (i + sa) % n_gx) * n_gy + (j + sb) % n_gy
                    perm.append((src, dst))
        pieces.append(lax.ppermute(packed[k], axes, perm))
    return pieces


def regrid(pieces, recv, weights, wet_rows):
    n_gx = lax.axis_size("gx")
    n_gy = lax.axis_size("gy")
    a = lax.axis_index("gx")
    b = lax.axis_index("gy")
    n_piece = len(pieces)
    cap, fld, tile = pieces[0].shape
    rows, refs = recv.shape
    source = recv // cap
    which = ((a - source // n_gy) % n_gx) * n_gy + (b - source % n_gy) % n_gy
    place = jnp.clip(recv % cap, 0, cap - 1)
    which = which.T.reshape(-1).astype(jnp.int32)
    place = place.T.reshape(-1).astype(jnp.int32)
    block = 16 if rows % 16 == 0 else rows
    steps = rows // block

    def kernel(which_ref, place_ref, *refs_in):
        piece_refs = refs_in[:n_piece]
        w_ref, wet_ref, out_ref, buf, sems = refs_in[n_piece:]
        i = pl.program_id(0)

        @pl.when(i == 0)
        def _():
            def issue(r, carry):
                k = r // rows
                x = r % rows
                p = which_ref[r]
                q = place_ref[r]
                for s in range(n_piece):
                    @pl.when(p == s)
                    def _():
                        pltpu.make_async_copy(
                            piece_refs[s].at[q], buf.at[k, x], sems.at[x // block]
                        ).start()
                return carry

            lax.fori_loop(0, rows * refs, issue, 0)

        def wait_one(r, carry):
            k = r // block
            x = i * block + r % block
            pltpu.make_async_copy(piece_refs[0].at[0], buf.at[k, x], sems.at[i]).wait()
            return carry

        lax.fori_loop(0, block * refs, wait_one, 0)
        acc = jnp.zeros((block, fld, tile), jnp.float32)
        for k in range(refs):
            src = buf[k, pl.ds(i * block, block)]
            acc = acc + lax.dot_general(
                src,
                w_ref[:, k],
                (((2,), (2,)), ((0,), (0,))),
                preferred_element_type=jnp.float32,
            )
        out_ref[...] = (acc * wet_ref[...][:, :, None]).astype(out_ref.dtype)

    grid_spec = pltpu.PrefetchScalarGridSpec(
        num_scalar_prefetch=2,
        grid=(steps,),
        in_specs=[pl.BlockSpec(memory_space=pl.ANY) for _ in range(n_piece)]
        + [
            pl.BlockSpec((block, refs, tile, tile), lambda i, w, q: (i, 0, 0, 0)),
            pl.BlockSpec((block, 1), lambda i, w, q: (i, 0)),
        ],
        out_specs=pl.BlockSpec((block, fld, tile), lambda i, w, q: (i, 0, 0)),
        scratch_shapes=[
            pltpu.VMEM((refs, rows, fld, tile), pieces[0].dtype),
            pltpu.SemaphoreType.DMA((steps,)),
        ],
    )
    return pl.pallas_call(
        kernel,
        grid_spec=grid_spec,
        out_shape=jax.ShapeDtypeStruct((rows, fld, tile), jnp.bfloat16),
        compiler_params=pltpu.CompilerParams(dimension_semantics=("arbitrary",)),
    )(which, place, *pieces, weights, wet_rows)


def per_device(
    state,
    velocity,
    diffusivity,
    export_proj,
    import_proj,
    intersection_weights,
    recv_slots,
    send_slots,
    land,
):
    highest = lax.Precision.HIGHEST
    section = lax.axis_index("comp")
    tracer = state[0]
    wet_tile = jnp.where(section == 0, jnp.ones(land.shape, jnp.float32), land.astype(jnp.float32))
    exports = (
        jnp.einsum("fl,lxy->xfy", export_proj[0], tracer, precision=highest) * wet_tile[:, :, None]
    ).astype(jnp.bfloat16)
    tables = send_slots[:, 0, 0]
    own_table = lax.dynamic_index_in_dim(tables, section, 0, keepdims=False)
    pieces = exchange(exports, own_table)
    imported = regrid(pieces, recv_slots[0, :, 0, :], intersection_weights[0, :, 0], wet_tile)
    wet_cells = wet_tile[None]
    for repeat in range(STEPS):
        tracer = advance(tracer, velocity[0], diffusivity[0], wet_cells)
    forcing = jnp.einsum(
        "lf,xfy->lxy", import_proj[0], imported.astype(jnp.float32), precision=highest
    )
    return ((tracer + wet_cells * forcing)[None], imported[None])


def solution(mesh):
    return jax.shard_map(
        per_device,
        mesh=mesh,
        in_specs=(
            P("comp", None, "gx", "gy"),
            P("comp", None, None, "gx", "gy"),
            P("comp", None),
            P("comp", None, None),
            P("comp", None, None),
            P("comp", "gx", "gy", None, None, None),
            P("comp", "gx", "gy", None),
            P(None, "gx", "gy", None, None),
            P("gx", "gy"),
        ),
        out_specs=(P("comp", None, "gx", "gy"), P("comp", "gx", None, "gy")),
        check_vma=False,
    )
```

```python
import jax
import jax.numpy as jnp
from jax import lax
from jax.sharding import PartitionSpec as P

STEPS = 2


def padded_2(cells, sides, width):
    for axis, dim in sides:
        count = lax.axis_size(axis)
        ends = count - 1
        head = lax.slice_in_dim(cells, 0, width, axis=dim)
        tail = lax.slice_in_dim(cells, cells.shape[dim] - width, cells.shape[dim], axis=dim)
        cells = jnp.concatenate(
            [
                lax.ppermute(tail, axis, [(i, (i + 1) % count) for i in range(ends)]),
                cells,
                lax.ppermute(head, axis, [((i + 1) % count, i) for i in range(ends)]),
            ],
            axis=dim,
        )
    return cells


def advance(tracer, speeds, coeffs, wet_mask):
    padded = padded_2(tracer.astype(jnp.bfloat16), (("gx", 1), ("gy", 2)), 1).astype(tracer.dtype)
    row_down = padded[:, 2:, 1:-1]
    row_up = padded[:, :-2, 1:-1]
    col_right = padded[:, 1:-1, 2:]
    col_left = padded[:, 1:-1, :-2]
    spread = row_down + row_up + col_right + col_left - 4.0 * tracer
    carried = 0.5 * (
        speeds[0].astype(jnp.float32) * (row_down - row_up)
        + speeds[1].astype(jnp.float32) * (col_right - col_left)
    )
    return tracer + wet_mask * (coeffs[:, None, None] * spread - carried)


def exchange(exports, own_table, recv):
    n_gx = lax.axis_size("gx")
    n_gy = lax.axis_size("gy")
    group = n_gx * n_gy
    cap = own_table.shape[1]
    section = lax.axis_index("comp")
    a = lax.axis_index("gx")
    b = lax.axis_index("gy")
    shifts = jnp.arange(group, dtype=jnp.int32)
    da = shifts // n_gy
    db = shifts % n_gy
    dest = ((a + da) % n_gx) * n_gy + (b + db) % n_gy
    packed = exports[own_table[dest]]
    axes = ("comp", "gx", "gy")
    cap_rows = cap * exports.shape[1]
    pieces = []
    for k in range(group):
        sa, sb = k // n_gy, k % n_gy
        perm = []
        for c in range(2):
            for i in range(n_gx):
                for j in range(n_gy):
                    src = (c * n_gx + i) * n_gy + j
                    dst = ((1 - c) * n_gx + (i + sa) % n_gx) * n_gy + (j + sb) % n_gy
                    perm.append((src, dst))
        pieces.append(lax.ppermute(packed[k].reshape(cap_rows, exports.shape[2]), axes, perm))
    arrived = jnp.concatenate(pieces, axis=0)
    source = recv // cap
    place = recv % cap
    k_of = ((a - source // n_gy) % n_gx) * n_gy + (b - source % n_gy) % n_gy
    return arrived.reshape(-1, exports.shape[1], exports.shape[2])[k_of * cap + place]


def per_device(
    state,
    velocity,
    diffusivity,
    export_proj,
    import_proj,
    intersection_weights,
    recv_slots,
    send_slots,
    land,
):
    highest = lax.Precision.HIGHEST
    section = lax.axis_index("comp")
    tracer = state[0]
    wet_tile = jnp.where(section == 0, jnp.ones(land.shape, jnp.float32), land.astype(jnp.float32))
    exports = (
        jnp.einsum("fl,lxy->xfy", export_proj[0], tracer, precision=highest) * wet_tile[:, :, None]
    ).astype(jnp.bfloat16)
    tables = send_slots[:, 0, 0]
    own_table = lax.dynamic_index_in_dim(tables, section, 0, keepdims=False)
    sources = exchange(exports, own_table, recv_slots[0, :, 0, :])
    summed = lax.dot_general(
        sources,
        intersection_weights[0, :, 0],
        (((1, 3), (1, 3)), ((0,), (0,))),
        preferred_element_type=jnp.float32,
    )
    imported = (summed * wet_tile[:, :, None]).astype(jnp.bfloat16)
    wet_cells = wet_tile[None]
    for repeat in range(STEPS):
        tracer = advance(tracer, velocity[0], diffusivity[0], wet_cells)
    forcing = jnp.einsum(
        "lf,xfy->lxy", import_proj[0], imported.astype(jnp.float32), precision=highest
    )
    return ((tracer + wet_cells * forcing)[None], imported[None])


def solution(mesh):
    return jax.shard_map(
        per_device,
        mesh=mesh,
        in_specs=(
            P("comp", None, "gx", "gy"),
            P("comp", None, None, "gx", "gy"),
            P("comp", None),
            P("comp", None, None),
            P("comp", None, None),
            P("comp", "gx", "gy", None, None, None),
            P("comp", "gx", "gy", None),
            P(None, "gx", "gy", None, None),
            P("gx", "gy"),
        ),
        out_specs=(P("comp", None, "gx", "gy"), P("comp", "gx", None, "gy")),
        check_vma=False,
    )
```

```python
import jax
import jax.numpy as jnp
from jax import lax
from jax.experimental import pallas as pl
from jax.experimental.pallas import tpu as pltpu
from jax.sharding import PartitionSpec as P

STEPS = 2


def padded_2(cells, sides, width):
    for axis, dim in sides:
        count = lax.axis_size(axis)
        ends = count - 1
        head = lax.slice_in_dim(cells, 0, width, axis=dim)
        tail = lax.slice_in_dim(cells, cells.shape[dim] - width, cells.shape[dim], axis=dim)
        cells = jnp.concatenate(
            [
                lax.ppermute(tail, axis, [(i, (i + 1) % count) for i in range(ends)]),
                cells,
                lax.ppermute(head, axis, [((i + 1) % count, i) for i in range(ends)]),
            ],
            axis=dim,
        )
    return cells


def advance(tracer, speeds, coeffs, wet_mask):
    padded = padded_2(tracer.astype(jnp.bfloat16), (("gx", 1), ("gy", 2)), 1).astype(tracer.dtype)
    row_down = padded[:, 2:, 1:-1]
    row_up = padded[:, :-2, 1:-1]
    col_right = padded[:, 1:-1, 2:]
    col_left = padded[:, 1:-1, :-2]
    spread = row_down + row_up + col_right + col_left - 4.0 * tracer
    carried = 0.5 * (
        speeds[0].astype(jnp.float32) * (row_down - row_up)
        + speeds[1].astype(jnp.float32) * (col_right - col_left)
    )
    return tracer + wet_mask * (coeffs[:, None, None] * spread - carried)


def exchange(exports, own_table):
    n_gx = lax.axis_size("gx")
    n_gy = lax.axis_size("gy")
    group = n_gx * n_gy
    a = lax.axis_index("gx")
    b = lax.axis_index("gy")
    shifts = jnp.arange(group, dtype=jnp.int32)
    dest = ((a + shifts // n_gy) % n_gx) * n_gy + (b + shifts % n_gy) % n_gy
    packed = exports[own_table[dest]]
    axes = ("comp", "gx", "gy")
    pieces = []
    for k in range(group):
        sa, sb = k // n_gy, k % n_gy
        perm = []
        for c in range(2):
            for i in range(n_gx):
                for j in range(n_gy):
                    src = (c * n_gx + i) * n_gy + j
                    dst = ((1 - c) * n_gx + (i + sa) % n_gx) * n_gy + (j + sb) % n_gy
                    perm.append((src, dst))
        pieces.append(lax.ppermute(packed[k], axes, perm))
    return pieces


def regrid(pieces, recv, weights, wet_rows):
    n_gx = lax.axis_size("gx")
    n_gy = lax.axis_size("gy")
    a = lax.axis_index("gx")
    b = lax.axis_index("gy")
    n_piece = len(pieces)
    cap, fld, tile = pieces[0].shape
    rows, refs = recv.shape
    source = recv // cap
    which = ((a - source // n_gy) % n_gx) * n_gy + (b - source % n_gy) % n_gy
    place = jnp.clip(recv % cap, 0, cap - 1)
    which = which.T.reshape(-1).astype(jnp.int32)
    place = place.T.reshape(-1).astype(jnp.int32)
    order = jnp.argsort(which, stable=True).astype(jnp.int32)
    place = place[order]
    counts = jnp.sum(which[None, :] == jnp.arange(n_piece, dtype=jnp.int32)[:, None], axis=1)
    bounds = jnp.concatenate([jnp.zeros((1,), jnp.int32), jnp.cumsum(counts).astype(jnp.int32)])
    block = 16 if rows % 16 == 0 else rows
    steps = rows // block

    def kernel(bounds_ref, order_ref, place_ref, *refs_in):
        piece_refs = refs_in[:n_piece]
        w_ref, wet_ref, out_ref, buf, sems = refs_in[n_piece:]
        i = pl.program_id(0)

        @pl.when(i == 0)
        def _():
            for s in range(n_piece):
                def issue(j, carry, s=s):
                    r = order_ref[j]
                    k = r // rows
                    x = r % rows
                    pltpu.make_async_copy(
                        piece_refs[s].at[place_ref[j]], buf.at[k, x], sems.at[x // block]
                    ).start()
                    return carry

                lax.fori_loop(bounds_ref[s], bounds_ref[s + 1], issue, 0)

        def wait_one(r, carry):
            k = r // block
            x = i * block + r % block
            pltpu.make_async_copy(piece_refs[0].at[0], buf.at[k, x], sems.at[i]).wait()
            return carry

        lax.fori_loop(0, block * refs, wait_one, 0)
        acc = jnp.zeros((block, fld, tile), jnp.float32)
        for k in range(refs):
            src = buf[k, pl.ds(i * block, block)]
            acc = acc + lax.dot_general(
                src,
                w_ref[:, k],
                (((2,), (2,)), ((0,), (0,))),
                preferred_element_type=jnp.float32,
            )
        out_ref[...] = (acc * wet_ref[...][:, :, None]).astype(out_ref.dtype)

    grid_spec = pltpu.PrefetchScalarGridSpec(
        num_scalar_prefetch=3,
        grid=(steps,),
        in_specs=[pl.BlockSpec(memory_space=pl.ANY) for _ in range(n_piece)]
        + [
            pl.BlockSpec((block, refs, tile, tile), lambda i, c, w, q: (i, 0, 0, 0)),
            pl.BlockSpec((block, 1), lambda i, c, w, q: (i, 0)),
        ],
        out_specs=pl.BlockSpec((block, fld, tile), lambda i, c, w, q: (i, 0, 0)),
        scratch_shapes=[
            pltpu.VMEM((refs, rows, fld, tile), pieces[0].dtype),
            pltpu.SemaphoreType.DMA((steps,)),
        ],
    )
    return pl.pallas_call(
        kernel,
        grid_spec=grid_spec,
        out_shape=jax.ShapeDtypeStruct((rows, fld, tile), jnp.bfloat16),
        compiler_params=pltpu.CompilerParams(dimension_semantics=("arbitrary",)),
    )(bounds, order, place, *pieces, weights, wet_rows)


def per_device(
    state,
    velocity,
    diffusivity,
    export_proj,
    import_proj,
    intersection_weights,
    recv_slots,
    send_slots,
    land,
):
    highest = lax.Precision.HIGHEST
    section = lax.axis_index("comp")
    tracer = state[0]
    wet_tile = jnp.where(section == 0, jnp.ones(land.shape, jnp.float32), land.astype(jnp.float32))
    exports = (
        jnp.einsum("fl,lxy->xfy", export_proj[0], tracer, precision=highest) * wet_tile[:, :, None]
    ).astype(jnp.bfloat16)
    tables = send_slots[:, 0, 0]
    own_table = lax.dynamic_index_in_dim(tables, section, 0, keepdims=False)
    pieces = exchange(exports, own_table)
    imported = regrid(pieces, recv_slots[0, :, 0, :], intersection_weights[0, :, 0], wet_tile)
    wet_cells = wet_tile[None]
    for repeat in range(STEPS):
        tracer = advance(tracer, velocity[0], diffusivity[0], wet_cells)
    forcing = jnp.einsum(
        "lf,xfy->lxy", import_proj[0], imported.astype(jnp.float32), precision=highest
    )
    return ((tracer + wet_cells * forcing)[None], imported[None])


def solution(mesh):
    return jax.shard_map(
        per_device,
        mesh=mesh,
        in_specs=(
            P("comp", None, "gx", "gy"),
            P("comp", None, None, "gx", "gy"),
            P("comp", None),
            P("comp", None, None),
            P("comp", None, None),
            P("comp", "gx", "gy", None, None, None),
            P("comp", "gx", "gy", None),
            P(None, "gx", "gy", None, None),
            P("gx", "gy"),
        ),
        out_specs=(P("comp", None, "gx", "gy"), P("comp", "gx", None, "gy")),
        check_vma=False,
    )
```

```python
import jax
import jax.numpy as jnp
from jax import lax
from jax.experimental import pallas as pl
from jax.experimental.pallas import tpu as pltpu
from jax.sharding import PartitionSpec as P

STEPS = 2


def padded_2(cells, sides, width):
    for axis, dim in sides:
        count = lax.axis_size(axis)
        ends = count - 1
        head = lax.slice_in_dim(cells, 0, width, axis=dim)
        tail = lax.slice_in_dim(cells, cells.shape[dim] - width, cells.shape[dim], axis=dim)
        cells = jnp.concatenate(
            [
                lax.ppermute(tail, axis, [(i, (i + 1) % count) for i in range(ends)]),
                cells,
                lax.ppermute(head, axis, [((i + 1) % count, i) for i in range(ends)]),
            ],
            axis=dim,
        )
    return cells


def advance(tracer, speeds, coeffs, wet_mask):
    padded = padded_2(tracer.astype(jnp.bfloat16), (("gx", 1), ("gy", 2)), 1).astype(tracer.dtype)
    row_down = padded[:, 2:, 1:-1]
    row_up = padded[:, :-2, 1:-1]
    col_right = padded[:, 1:-1, 2:]
    col_left = padded[:, 1:-1, :-2]
    spread = row_down + row_up + col_right + col_left - 4.0 * tracer
    carried = 0.5 * (
        speeds[0].astype(jnp.float32) * (row_down - row_up)
        + speeds[1].astype(jnp.float32) * (col_right - col_left)
    )
    return tracer + wet_mask * (coeffs[:, None, None] * spread - carried)


def exchange(exports, own_table):
    n_gx = lax.axis_size("gx")
    n_gy = lax.axis_size("gy")
    group = n_gx * n_gy
    a = lax.axis_index("gx")
    b = lax.axis_index("gy")
    shifts = jnp.arange(group, dtype=jnp.int32)
    dest = ((a + shifts // n_gy) % n_gx) * n_gy + (b + shifts % n_gy) % n_gy
    packed = exports[own_table[dest]]
    axes = ("comp", "gx", "gy")
    pieces = []
    for k in range(group):
        sa, sb = k // n_gy, k % n_gy
        perm = []
        for c in range(2):
            for i in range(n_gx):
                for j in range(n_gy):
                    src = (c * n_gx + i) * n_gy + j
                    dst = ((1 - c) * n_gx + (i + sa) % n_gx) * n_gy + (j + sb) % n_gy
                    perm.append((src, dst))
        pieces.append(lax.ppermute(packed[k], axes, perm))
    return pieces


def regrid(pieces, recv, weights, wet_rows):
    n_gx = lax.axis_size("gx")
    n_gy = lax.axis_size("gy")
    a = lax.axis_index("gx")
    b = lax.axis_index("gy")
    n_piece = len(pieces)
    cap, fld, tile = pieces[0].shape
    rows, refs = recv.shape
    source = recv // cap
    which = ((a - source // n_gy) % n_gx) * n_gy + (b - source % n_gy) % n_gy
    place = jnp.clip(recv % cap, 0, cap - 1)
    which = which.T.reshape(-1).astype(jnp.int32)
    place = place.T.reshape(-1).astype(jnp.int32)
    order = jnp.argsort(which, stable=True).astype(jnp.int32)
    place = place[order]
    counts = jnp.sum(which[None, :] == jnp.arange(n_piece, dtype=jnp.int32)[:, None], axis=1)
    bounds = jnp.concatenate([jnp.zeros((1,), jnp.int32), jnp.cumsum(counts).astype(jnp.int32)])

    def kernel(bounds_ref, order_ref, place_ref, *refs_in):
        piece_refs = refs_in[:n_piece]
        out_ref, sem = refs_in[n_piece:]
        for s in range(n_piece):
            def issue(j, carry, s=s):
                r = order_ref[j]
                pltpu.make_async_copy(
                    piece_refs[s].at[place_ref[j]], out_ref.at[r // rows, r % rows], sem
                ).start()
                return carry

            lax.fori_loop(bounds_ref[s], bounds_ref[s + 1], issue, 0)

        def wait_one(r, carry):
            pltpu.make_async_copy(
                piece_refs[0].at[0], out_ref.at[r // rows, r % rows], sem
            ).wait()
            return carry

        lax.fori_loop(0, rows * refs, wait_one, 0)

    grid_spec = pltpu.PrefetchScalarGridSpec(
        num_scalar_prefetch=3,
        grid=(1,),
        in_specs=[pl.BlockSpec(memory_space=pl.ANY) for _ in range(n_piece)],
        out_specs=pl.BlockSpec((refs, rows, fld, tile), lambda i, c, w, q: (0, 0, 0, 0)),
        scratch_shapes=[pltpu.SemaphoreType.DMA(())],
    )
    sources = pl.pallas_call(
        kernel,
        grid_spec=grid_spec,
        out_shape=jax.ShapeDtypeStruct((refs, rows, fld, tile), pieces[0].dtype),
    )(bounds, order, place, *pieces)
    summed = lax.dot_general(
        sources,
        weights,
        (((0, 3), (1, 3)), ((1,), (0,))),
        preferred_element_type=jnp.float32,
    )
    return (summed * wet_rows[:, :, None]).astype(jnp.bfloat16)


def per_device(
    state,
    velocity,
    diffusivity,
    export_proj,
    import_proj,
    intersection_weights,
    recv_slots,
    send_slots,
    land,
):
    highest = lax.Precision.HIGHEST
    section = lax.axis_index("comp")
    tracer = state[0]
    wet_tile = jnp.where(section == 0, jnp.ones(land.shape, jnp.float32), land.astype(jnp.float32))
    exports = (
        jnp.einsum("fl,lxy->xfy", export_proj[0], tracer, precision=highest) * wet_tile[:, :, None]
    ).astype(jnp.bfloat16)
    tables = send_slots[:, 0, 0]
    own_table = lax.dynamic_index_in_dim(tables, section, 0, keepdims=False)
    pieces = exchange(exports, own_table)
    imported = regrid(pieces, recv_slots[0, :, 0, :], intersection_weights[0, :, 0], wet_tile)
    wet_cells = wet_tile[None]
    for repeat in range(STEPS):
        tracer = advance(tracer, velocity[0], diffusivity[0], wet_cells)
    forcing = jnp.einsum(
        "lf,xfy->lxy", import_proj[0], imported.astype(jnp.float32), precision=highest
    )
    return ((tracer + wet_cells * forcing)[None], imported[None])


def solution(mesh):
    return jax.shard_map(
        per_device,
        mesh=mesh,
        in_specs=(
            P("comp", None, "gx", "gy"),
            P("comp", None, None, "gx", "gy"),
            P("comp", None),
            P("comp", None, None),
            P("comp", None, None),
            P("comp", "gx", "gy", None, None, None),
            P("comp", "gx", "gy", None),
            P(None, "gx", "gy", None, None),
            P("gx", "gy"),
        ),
        out_specs=(P("comp", None, "gx", "gy"), P("comp", "gx", None, "gy")),
        check_vma=False,
    )
```

```python
import jax
import jax.numpy as jnp
from jax import lax
from jax.experimental import pallas as pl
from jax.experimental.pallas import tpu as pltpu
from jax.sharding import PartitionSpec as P

STEPS = 2


def padded_2(cells, sides, width):
    for axis, dim in sides:
        count = lax.axis_size(axis)
        ends = count - 1
        head = lax.slice_in_dim(cells, 0, width, axis=dim)
        tail = lax.slice_in_dim(cells, cells.shape[dim] - width, cells.shape[dim], axis=dim)
        cells = jnp.concatenate(
            [
                lax.ppermute(tail, axis, [(i, (i + 1) % count) for i in range(ends)]),
                cells,
                lax.ppermute(head, axis, [((i + 1) % count, i) for i in range(ends)]),
            ],
            axis=dim,
        )
    return cells


def advance(tracer, speeds, coeffs, wet_mask):
    padded = padded_2(tracer.astype(jnp.bfloat16), (("gx", 1), ("gy", 2)), 1).astype(tracer.dtype)
    row_down = padded[:, 2:, 1:-1]
    row_up = padded[:, :-2, 1:-1]
    col_right = padded[:, 1:-1, 2:]
    col_left = padded[:, 1:-1, :-2]
    spread = row_down + row_up + col_right + col_left - 4.0 * tracer
    carried = 0.5 * (
        speeds[0].astype(jnp.float32) * (row_down - row_up)
        + speeds[1].astype(jnp.float32) * (col_right - col_left)
    )
    return tracer + wet_mask * (coeffs[:, None, None] * spread - carried)


def exchange(exports, own_table):
    n_gx = lax.axis_size("gx")
    n_gy = lax.axis_size("gy")
    group = n_gx * n_gy
    a = lax.axis_index("gx")
    b = lax.axis_index("gy")
    shifts = jnp.arange(group, dtype=jnp.int32)
    dest = ((a + shifts // n_gy) % n_gx) * n_gy + (b + shifts % n_gy) % n_gy
    packed = exports[own_table[dest]]
    axes = ("comp", "gx", "gy")
    pieces = []
    for k in range(group):
        sa, sb = k // n_gy, k % n_gy
        perm = []
        for c in range(2):
            for i in range(n_gx):
                for j in range(n_gy):
                    src = (c * n_gx + i) * n_gy + j
                    dst = ((1 - c) * n_gx + (i + sa) % n_gx) * n_gy + (j + sb) % n_gy
                    perm.append((src, dst))
        pieces.append(lax.ppermute(packed[k], axes, perm))
    return pieces


def regrid(pieces, recv, weights, wet_rows):
    n_gx = lax.axis_size("gx")
    n_gy = lax.axis_size("gy")
    a = lax.axis_index("gx")
    b = lax.axis_index("gy")
    n_piece = len(pieces)
    cap, fld, tile = pieces[0].shape
    rows, refs = recv.shape
    source = recv // cap
    which = ((a - source // n_gy) % n_gx) * n_gy + (b - source % n_gy) % n_gy
    place = jnp.clip(recv % cap, 0, cap - 1)
    which = which.T.reshape(-1).astype(jnp.int32)
    place = place.T.reshape(-1).astype(jnp.int32)
    order = jnp.argsort(which, stable=True).astype(jnp.int32)
    counts = jnp.sum(which[None, :] == jnp.arange(n_piece, dtype=jnp.int32)[:, None], axis=1)
    bounds = jnp.concatenate([jnp.zeros((1,), jnp.int32), jnp.cumsum(counts).astype(jnp.int32)])

    def kernel(bounds_ref, order_ref, place_ref, *refs_in):
        piece_refs = refs_in[:n_piece]
        out_ref = refs_in[n_piece]
        for s in range(n_piece):
            def copy_one(j, carry, s=s):
                r = order_ref[j]
                out_ref[r // rows, r % rows] = piece_refs[s][place_ref[r]]
                return carry

            lax.fori_loop(bounds_ref[s], bounds_ref[s + 1], copy_one, 0)

    grid_spec = pltpu.PrefetchScalarGridSpec(
        num_scalar_prefetch=3,
        grid=(1,),
        in_specs=[
            pl.BlockSpec((cap, fld, tile), lambda i, c, w, q: (0, 0, 0)) for _ in range(n_piece)
        ],
        out_specs=pl.BlockSpec((refs, rows, fld, tile), lambda i, c, w, q: (0, 0, 0, 0)),
    )
    sources = pl.pallas_call(
        kernel,
        grid_spec=grid_spec,
        out_shape=jax.ShapeDtypeStruct((refs, rows, fld, tile), pieces[0].dtype),
    )(bounds, order, place, *pieces)
    summed = lax.dot_general(
        sources,
        weights,
        (((0, 3), (1, 3)), ((1,), (0,))),
        preferred_element_type=jnp.float32,
    )
    return (summed * wet_rows[:, :, None]).astype(jnp.bfloat16)


def per_device(
    state,
    velocity,
    diffusivity,
    export_proj,
    import_proj,
    intersection_weights,
    recv_slots,
    send_slots,
    land,
):
    highest = lax.Precision.HIGHEST
    section = lax.axis_index("comp")
    tracer = state[0]
    wet_tile = jnp.where(section == 0, jnp.ones(land.shape, jnp.float32), land.astype(jnp.float32))
    exports = (
        jnp.einsum("fl,lxy->xfy", export_proj[0], tracer, precision=highest) * wet_tile[:, :, None]
    ).astype(jnp.bfloat16)
    tables = send_slots[:, 0, 0]
    own_table = lax.dynamic_index_in_dim(tables, section, 0, keepdims=False)
    pieces = exchange(exports, own_table)
    imported = regrid(pieces, recv_slots[0, :, 0, :], intersection_weights[0, :, 0], wet_tile)
    wet_cells = wet_tile[None]
    for repeat in range(STEPS):
        tracer = advance(tracer, velocity[0], diffusivity[0], wet_cells)
    imported_f = imported.astype(jnp.float32)
    forcing = sum(
        import_proj[0][:, f, None, None] * imported_f[None, :, f, :]
        for f in range(imported.shape[1])
    )
    return ((tracer + wet_cells * forcing)[None], imported[None])


def solution(mesh):
    return jax.shard_map(
        per_device,
        mesh=mesh,
        in_specs=(
            P("comp", None, "gx", "gy"),
            P("comp", None, None, "gx", "gy"),
            P("comp", None),
            P("comp", None, None),
            P("comp", None, None),
            P("comp", "gx", "gy", None, None, None),
            P("comp", "gx", "gy", None),
            P(None, "gx", "gy", None, None),
            P("gx", "gy"),
        ),
        out_specs=(P("comp", None, "gx", "gy"), P("comp", "gx", None, "gy")),
        check_vma=False,
    )
```

```python
import jax
import jax.numpy as jnp
from jax import lax
from jax.experimental import pallas as pl
from jax.experimental.pallas import tpu as pltpu
from jax.sharding import PartitionSpec as P

STEPS = 2


def padded_2(cells, sides, width):
    for axis, dim in sides:
        count = lax.axis_size(axis)
        ends = count - 1
        head = lax.slice_in_dim(cells, 0, width, axis=dim)
        tail = lax.slice_in_dim(cells, cells.shape[dim] - width, cells.shape[dim], axis=dim)
        cells = jnp.concatenate(
            [
                lax.ppermute(tail, axis, [(i, (i + 1) % count) for i in range(ends)]),
                cells,
                lax.ppermute(head, axis, [((i + 1) % count, i) for i in range(ends)]),
            ],
            axis=dim,
        )
    return cells


def advance(tracer, speeds, coeffs, wet_mask):
    padded = padded_2(tracer.astype(jnp.bfloat16), (("gx", 1), ("gy", 2)), 1).astype(tracer.dtype)
    row_down = padded[:, 2:, 1:-1]
    row_up = padded[:, :-2, 1:-1]
    col_right = padded[:, 1:-1, 2:]
    col_left = padded[:, 1:-1, :-2]
    spread = row_down + row_up + col_right + col_left - 4.0 * tracer
    carried = 0.5 * (
        speeds[0].astype(jnp.float32) * (row_down - row_up)
        + speeds[1].astype(jnp.float32) * (col_right - col_left)
    )
    return tracer + wet_mask * (coeffs[:, None, None] * spread - carried)


def exchange(exports, own_table):
    n_gx = lax.axis_size("gx")
    n_gy = lax.axis_size("gy")
    group = n_gx * n_gy
    a = lax.axis_index("gx")
    b = lax.axis_index("gy")
    shifts = jnp.arange(group, dtype=jnp.int32)
    dest = ((a + shifts // n_gy) % n_gx) * n_gy + (b + shifts % n_gy) % n_gy
    packed = exports[own_table[dest]]
    axes = ("comp", "gx", "gy")
    pieces = []
    for k in range(group):
        sa, sb = k // n_gy, k % n_gy
        perm = []
        for c in range(2):
            for i in range(n_gx):
                for j in range(n_gy):
                    src = (c * n_gx + i) * n_gy + j
                    dst = ((1 - c) * n_gx + (i + sa) % n_gx) * n_gy + (j + sb) % n_gy
                    perm.append((src, dst))
        pieces.append(lax.ppermute(packed[k], axes, perm))
    return pieces


def regrid(pieces, recv, weights, wet_rows):
    n_gx = lax.axis_size("gx")
    n_gy = lax.axis_size("gy")
    a = lax.axis_index("gx")
    b = lax.axis_index("gy")
    n_piece = len(pieces)
    cap, fld, tile = pieces[0].shape
    rows, refs = recv.shape
    source = recv // cap
    which = ((a - source // n_gy) % n_gx) * n_gy + (b - source % n_gy) % n_gy
    place = jnp.clip(recv % cap, 0, cap - 1)
    which = which.T.reshape(-1).astype(jnp.int32)
    place = place.T.reshape(-1).astype(jnp.int32)
    order = jnp.argsort(which, stable=True).astype(jnp.int32)
    counts = jnp.sum(which[None, :] == jnp.arange(n_piece, dtype=jnp.int32)[:, None], axis=1)
    bounds = jnp.concatenate([jnp.zeros((1,), jnp.int32), jnp.cumsum(counts).astype(jnp.int32)])

    def kernel(bounds_ref, order_ref, place_ref, *refs_in):
        piece_refs = refs_in[:n_piece]
        out_ref = refs_in[n_piece]
        for s in range(n_piece):
            def copy_one(j, carry, s=s):
                r = order_ref[j]
                out_ref[r // rows, r % rows] = piece_refs[s][place_ref[r]]
                return carry

            lax.fori_loop(bounds_ref[s], bounds_ref[s + 1], copy_one, 0)

    grid_spec = pltpu.PrefetchScalarGridSpec(
        num_scalar_prefetch=3,
        grid=(1,),
        in_specs=[
            pl.BlockSpec((cap, fld, tile), lambda i, c, w, q: (0, 0, 0)) for _ in range(n_piece)
        ],
        out_specs=pl.BlockSpec((refs, rows, fld, tile), lambda i, c, w, q: (0, 0, 0, 0)),
    )
    sources = pl.pallas_call(
        kernel,
        grid_spec=grid_spec,
        out_shape=jax.ShapeDtypeStruct((refs, rows, fld, tile), pieces[0].dtype),
    )(bounds, order, place, *pieces)
    summed = lax.dot_general(
        sources,
        weights,
        (((0, 3), (1, 3)), ((1,), (0,))),
        preferred_element_type=jnp.float32,
    )
    return (summed * wet_rows[:, :, None]).astype(jnp.bfloat16)


def per_device(
    state,
    velocity,
    diffusivity,
    export_proj,
    import_proj,
    intersection_weights,
    recv_slots,
    send_slots,
    land,
):
    highest = lax.Precision.HIGHEST
    section = lax.axis_index("comp")
    tracer = state[0]
    wet_tile = jnp.where(section == 0, jnp.ones(land.shape, jnp.float32), land.astype(jnp.float32))
    exports = (
        jnp.einsum("fl,lxy->xfy", export_proj[0], tracer, precision=highest) * wet_tile[:, :, None]
    ).astype(jnp.bfloat16)
    tables = send_slots[:, 0, 0]
    own_table = lax.dynamic_index_in_dim(tables, section, 0, keepdims=False)
    pieces = exchange(exports, own_table)
    imported = regrid(pieces, recv_slots[0, :, 0, :], intersection_weights[0, :, 0], wet_tile)
    wet_cells = wet_tile[None]
    for repeat in range(STEPS):
        tracer = advance(tracer, velocity[0], diffusivity[0], wet_cells)
    forcing = jnp.einsum(
        "lf,xfy->lxy", import_proj[0], imported.astype(jnp.float32), precision=highest
    )
    return ((tracer + wet_cells * forcing)[None], imported[None])


def solution(mesh):
    return jax.shard_map(
        per_device,
        mesh=mesh,
        in_specs=(
            P("comp", None, "gx", "gy"),
            P("comp", None, None, "gx", "gy"),
            P("comp", None),
            P("comp", None, None),
            P("comp", None, None),
            P("comp", "gx", "gy", None, None, None),
            P("comp", "gx", "gy", None),
            P(None, "gx", "gy", None, None),
            P("gx", "gy"),
        ),
        out_specs=(P("comp", None, "gx", "gy"), P("comp", "gx", None, "gy")),
        check_vma=False,
    )
```

```python
import jax
import jax.numpy as jnp
from jax import lax
from jax.experimental import pallas as pl
from jax.experimental.pallas import tpu as pltpu
from jax.sharding import PartitionSpec as P

STEPS = 2


def padded_2(cells, sides, width):
    for axis, dim in sides:
        count = lax.axis_size(axis)
        ends = count - 1
        head = lax.slice_in_dim(cells, 0, width, axis=dim)
        tail = lax.slice_in_dim(cells, cells.shape[dim] - width, cells.shape[dim], axis=dim)
        cells = jnp.concatenate(
            [
                lax.ppermute(tail, axis, [(i, (i + 1) % count) for i in range(ends)]),
                cells,
                lax.ppermute(head, axis, [((i + 1) % count, i) for i in range(ends)]),
            ],
            axis=dim,
        )
    return cells


def advance(tracer, speeds, coeffs, wet_mask):
    padded = padded_2(tracer.astype(jnp.bfloat16), (("gx", 1), ("gy", 2)), 1).astype(tracer.dtype)
    row_down = padded[:, 2:, 1:-1]
    row_up = padded[:, :-2, 1:-1]
    col_right = padded[:, 1:-1, 2:]
    col_left = padded[:, 1:-1, :-2]
    spread = row_down + row_up + col_right + col_left - 4.0 * tracer
    carried = 0.5 * (
        speeds[0].astype(jnp.float32) * (row_down - row_up)
        + speeds[1].astype(jnp.float32) * (col_right - col_left)
    )
    return tracer + wet_mask * (coeffs[:, None, None] * spread - carried)


def exchange(exports, own_table):
    n_gx = lax.axis_size("gx")
    n_gy = lax.axis_size("gy")
    group = n_gx * n_gy
    a = lax.axis_index("gx")
    b = lax.axis_index("gy")
    shifts = jnp.arange(group, dtype=jnp.int32)
    dest = ((a + shifts // n_gy) % n_gx) * n_gy + (b + shifts % n_gy) % n_gy
    packed = exports[own_table[dest]]
    axes = ("comp", "gx", "gy")
    pieces = []
    for k in range(group):
        sa, sb = k // n_gy, k % n_gy
        perm = []
        for c in range(2):
            for i in range(n_gx):
                for j in range(n_gy):
                    src = (c * n_gx + i) * n_gy + j
                    dst = ((1 - c) * n_gx + (i + sa) % n_gx) * n_gy + (j + sb) % n_gy
                    perm.append((src, dst))
        pieces.append(lax.ppermute(packed[k], axes, perm))
    return pieces


def regrid(pieces, recv, weights, wet_rows):
    n_gx = lax.axis_size("gx")
    n_gy = lax.axis_size("gy")
    a = lax.axis_index("gx")
    b = lax.axis_index("gy")
    n_piece = len(pieces)
    cap, fld, tile = pieces[0].shape
    rows, refs = recv.shape
    source = recv // cap
    which = ((a - source // n_gy) % n_gx) * n_gy + (b - source % n_gy) % n_gy
    place = jnp.clip(recv % cap, 0, cap - 1)
    which = which.T.reshape(-1).astype(jnp.int32)
    place = place.T.reshape(-1).astype(jnp.int32)

    def kernel(which_ref, place_ref, *refs_in):
        piece_refs = refs_in[:n_piece]
        out_ref, buf, sems = refs_in[n_piece:]
        copies = [
            pltpu.make_async_copy(piece_refs[s], buf.at[s], sems.at[s]) for s in range(n_piece)
        ]
        for c in copies:
            c.start()
        for c in copies:
            c.wait()

        def copy_one(r, carry):
            out_ref[r // rows, r % rows] = buf[which_ref[r], place_ref[r]]
            return carry

        lax.fori_loop(0, rows * refs, copy_one, 0)

    grid_spec = pltpu.PrefetchScalarGridSpec(
        num_scalar_prefetch=2,
        grid=(1,),
        in_specs=[pl.BlockSpec(memory_space=pl.ANY) for _ in range(n_piece)],
        out_specs=pl.BlockSpec((refs, rows, fld, tile), lambda i, w, q: (0, 0, 0, 0)),
        scratch_shapes=[
            pltpu.VMEM((n_piece, cap, fld, tile), pieces[0].dtype),
            pltpu.SemaphoreType.DMA((n_piece,)),
        ],
    )
    sources = pl.pallas_call(
        kernel,
        grid_spec=grid_spec,
        out_shape=jax.ShapeDtypeStruct((refs, rows, fld, tile), pieces[0].dtype),
    )(which, place, *pieces)
    summed = lax.dot_general(
        sources,
        weights,
        (((0, 3), (1, 3)), ((1,), (0,))),
        preferred_element_type=jnp.float32,
    )
    return (summed * wet_rows[:, :, None]).astype(jnp.bfloat16)


def per_device(
    state,
    velocity,
    diffusivity,
    export_proj,
    import_proj,
    intersection_weights,
    recv_slots,
    send_slots,
    land,
):
    highest = lax.Precision.HIGHEST
    section = lax.axis_index("comp")
    tracer = state[0]
    wet_tile = jnp.where(section == 0, jnp.ones(land.shape, jnp.float32), land.astype(jnp.float32))
    exports = (
        jnp.einsum("fl,lxy->xfy", export_proj[0], tracer, precision=highest) * wet_tile[:, :, None]
    ).astype(jnp.bfloat16)
    tables = send_slots[:, 0, 0]
    own_table = lax.dynamic_index_in_dim(tables, section, 0, keepdims=False)
    pieces = exchange(exports, own_table)
    imported = regrid(pieces, recv_slots[0, :, 0, :], intersection_weights[0, :, 0], wet_tile)
    wet_cells = wet_tile[None]
    for repeat in range(STEPS):
        tracer = advance(tracer, velocity[0], diffusivity[0], wet_cells)
    forcing = jnp.einsum(
        "lf,xfy->lxy", import_proj[0], imported.astype(jnp.float32), precision=highest
    )
    return ((tracer + wet_cells * forcing)[None], imported[None])


def solution(mesh):
    return jax.shard_map(
        per_device,
        mesh=mesh,
        in_specs=(
            P("comp", None, "gx", "gy"),
            P("comp", None, None, "gx", "gy"),
            P("comp", None),
            P("comp", None, None),
            P("comp", None, None),
            P("comp", "gx", "gy", None, None, None),
            P("comp", "gx", "gy", None),
            P(None, "gx", "gy", None, None),
            P("gx", "gy"),
        ),
        out_specs=(P("comp", None, "gx", "gy"), P("comp", "gx", None, "gy")),
        check_vma=False,
    )
```

```python
import jax
import jax.numpy as jnp
from jax import lax
from jax.experimental import pallas as pl
from jax.experimental.pallas import tpu as pltpu
from jax.sharding import PartitionSpec as P

STEPS = 2


def padded_2(cells, sides, width):
    for axis, dim in sides:
        count = lax.axis_size(axis)
        ends = count - 1
        head = lax.slice_in_dim(cells, 0, width, axis=dim)
        tail = lax.slice_in_dim(cells, cells.shape[dim] - width, cells.shape[dim], axis=dim)
        cells = jnp.concatenate(
            [
                lax.ppermute(tail, axis, [(i, (i + 1) % count) for i in range(ends)]),
                cells,
                lax.ppermute(head, axis, [((i + 1) % count, i) for i in range(ends)]),
            ],
            axis=dim,
        )
    return cells


def advance(tracer, speeds, coeffs, wet_mask):
    padded = padded_2(tracer.astype(jnp.bfloat16), (("gx", 1), ("gy", 2)), 1).astype(tracer.dtype)
    row_down = padded[:, 2:, 1:-1]
    row_up = padded[:, :-2, 1:-1]
    col_right = padded[:, 1:-1, 2:]
    col_left = padded[:, 1:-1, :-2]
    spread = row_down + row_up + col_right + col_left - 4.0 * tracer
    carried = 0.5 * (
        speeds[0].astype(jnp.float32) * (row_down - row_up)
        + speeds[1].astype(jnp.float32) * (col_right - col_left)
    )
    return tracer + wet_mask * (coeffs[:, None, None] * spread - carried)


def exchange(exports, own_table):
    n_gx = lax.axis_size("gx")
    n_gy = lax.axis_size("gy")
    group = n_gx * n_gy
    a = lax.axis_index("gx")
    b = lax.axis_index("gy")
    shifts = jnp.arange(group, dtype=jnp.int32)
    dest = ((a + shifts // n_gy) % n_gx) * n_gy + (b + shifts % n_gy) % n_gy
    packed = exports[own_table[dest]]
    axes = ("comp", "gx", "gy")
    pieces = []
    for k in range(group):
        sa, sb = k // n_gy, k % n_gy
        perm = []
        for c in range(2):
            for i in range(n_gx):
                for j in range(n_gy):
                    src = (c * n_gx + i) * n_gy + j
                    dst = ((1 - c) * n_gx + (i + sa) % n_gx) * n_gy + (j + sb) % n_gy
                    perm.append((src, dst))
        pieces.append(lax.ppermute(packed[k], axes, perm))
    return pieces


def regrid(pieces, recv, weights, wet_rows):
    n_gx = lax.axis_size("gx")
    n_gy = lax.axis_size("gy")
    a = lax.axis_index("gx")
    b = lax.axis_index("gy")
    n_piece = len(pieces)
    cap, fld, tile = pieces[0].shape
    rows, refs = recv.shape
    source = recv // cap
    which = ((a - source // n_gy) % n_gx) * n_gy + (b - source % n_gy) % n_gy
    place = jnp.clip(recv % cap, 0, cap - 1)
    which = which.T.reshape(-1).astype(jnp.int32)
    place = place.T.reshape(-1).astype(jnp.int32)

    def kernel(which_ref, place_ref, *refs_in):
        piece_refs = refs_in[:n_piece]
        out_ref, buf, sems = refs_in[n_piece:]
        copies = [
            pltpu.make_async_copy(piece_refs[s], buf.at[s], sems.at[s]) for s in range(n_piece)
        ]
        for c in copies:
            c.start()
        for c in copies:
            c.wait()

        def copy_one(r, carry):
            out_ref[r // rows, r % rows] = buf[which_ref[r], place_ref[r]]
            return carry

        lax.fori_loop(0, rows * refs, copy_one, 0, unroll=8)

    grid_spec = pltpu.PrefetchScalarGridSpec(
        num_scalar_prefetch=2,
        grid=(1,),
        in_specs=[pl.BlockSpec(memory_space=pl.ANY) for _ in range(n_piece)],
        out_specs=pl.BlockSpec((refs, rows, fld, tile), lambda i, w, q: (0, 0, 0, 0)),
        scratch_shapes=[
            pltpu.VMEM((n_piece, cap, fld, tile), pieces[0].dtype),
            pltpu.SemaphoreType.DMA((n_piece,)),
        ],
    )
    sources = pl.pallas_call(
        kernel,
        grid_spec=grid_spec,
        out_shape=jax.ShapeDtypeStruct((refs, rows, fld, tile), pieces[0].dtype),
    )(which, place, *pieces)
    summed = lax.dot_general(
        sources,
        weights,
        (((0, 3), (1, 3)), ((1,), (0,))),
        preferred_element_type=jnp.float32,
    )
    return (summed * wet_rows[:, :, None]).astype(jnp.bfloat16)


def per_device(
    state,
    velocity,
    diffusivity,
    export_proj,
    import_proj,
    intersection_weights,
    recv_slots,
    send_slots,
    land,
):
    highest = lax.Precision.HIGHEST
    section = lax.axis_index("comp")
    tracer = state[0]
    wet_tile = jnp.where(section == 0, jnp.ones(land.shape, jnp.float32), land.astype(jnp.float32))
    exports = (
        jnp.einsum("fl,lxy->xfy", export_proj[0], tracer, precision=highest) * wet_tile[:, :, None]
    ).astype(jnp.bfloat16)
    tables = send_slots[:, 0, 0]
    own_table = lax.dynamic_index_in_dim(tables, section, 0, keepdims=False)
    pieces = exchange(exports, own_table)
    imported = regrid(pieces, recv_slots[0, :, 0, :], intersection_weights[0, :, 0], wet_tile)
    wet_cells = wet_tile[None]
    for repeat in range(STEPS):
        tracer = advance(tracer, velocity[0], diffusivity[0], wet_cells)
    forcing = jnp.einsum(
        "lf,xfy->lxy", import_proj[0], imported.astype(jnp.float32), precision=highest
    )
    return ((tracer + wet_cells * forcing)[None], imported[None])


def solution(mesh):
    return jax.shard_map(
        per_device,
        mesh=mesh,
        in_specs=(
            P("comp", None, "gx", "gy"),
            P("comp", None, None, "gx", "gy"),
            P("comp", None),
            P("comp", None, None),
            P("comp", None, None),
            P("comp", "gx", "gy", None, None, None),
            P("comp", "gx", "gy", None),
            P(None, "gx", "gy", None, None),
            P("gx", "gy"),
        ),
        out_specs=(P("comp", None, "gx", "gy"), P("comp", "gx", None, "gy")),
        check_vma=False,
    )
```

```python
import jax
import jax.numpy as jnp
from jax import lax
from jax.experimental import pallas as pl
from jax.experimental.pallas import tpu as pltpu
from jax.sharding import PartitionSpec as P

STEPS = 2


def padded_2(cells, sides, width):
    for axis, dim in sides:
        count = lax.axis_size(axis)
        ends = count - 1
        head = lax.slice_in_dim(cells, 0, width, axis=dim)
        tail = lax.slice_in_dim(cells, cells.shape[dim] - width, cells.shape[dim], axis=dim)
        cells = jnp.concatenate(
            [
                lax.ppermute(tail, axis, [(i, (i + 1) % count) for i in range(ends)]),
                cells,
                lax.ppermute(head, axis, [((i + 1) % count, i) for i in range(ends)]),
            ],
            axis=dim,
        )
    return cells


def advance(tracer, speeds, coeffs, wet_mask):
    padded = padded_2(tracer.astype(jnp.bfloat16), (("gx", 1), ("gy", 2)), 1).astype(tracer.dtype)
    row_down = padded[:, 2:, 1:-1]
    row_up = padded[:, :-2, 1:-1]
    col_right = padded[:, 1:-1, 2:]
    col_left = padded[:, 1:-1, :-2]
    spread = row_down + row_up + col_right + col_left - 4.0 * tracer
    carried = 0.5 * (
        speeds[0].astype(jnp.float32) * (row_down - row_up)
        + speeds[1].astype(jnp.float32) * (col_right - col_left)
    )
    return tracer + wet_mask * (coeffs[:, None, None] * spread - carried)


def swap(parts, axis):
    count = lax.axis_size(axis)
    ends = count - 1
    heads = [lax.slice_in_dim(x, 0, w, axis=d) for x, d, w in parts]
    tails = [lax.slice_in_dim(x, x.shape[d] - w, x.shape[d], axis=d) for x, d, w in parts]

    def send(slabs, perm):
        flat = jnp.concatenate([s.astype(jnp.float32).reshape(-1) for s in slabs])
        got = lax.ppermute(flat, axis, perm)
        out, at = [], 0
        for s in slabs:
            out.append(got[at:at + s.size].reshape(s.shape))
            at += s.size
        return out

    from_prev = send(tails, [(i, i + 1) for i in range(ends)])
    from_next = send(heads, [(i + 1, i) for i in range(ends)])
    return [
        jnp.concatenate([p, x.astype(jnp.float32), n], axis=d)
        for (x, d, w), p, n in zip(parts, from_prev, from_next)
    ]


def step(ext, speeds, coeffs, wet_mask):
    centre = ext[:, 1:-1, 1:-1]
    row_down = ext[:, 2:, 1:-1]
    row_up = ext[:, :-2, 1:-1]
    col_right = ext[:, 1:-1, 2:]
    col_left = ext[:, 1:-1, :-2]
    spread = row_down + row_up + col_right + col_left - 4.0 * centre
    carried = 0.5 * (
        speeds[0].astype(jnp.float32) * (row_down - row_up)
        + speeds[1].astype(jnp.float32) * (col_right - col_left)
    )
    return centre + wet_mask * (coeffs[:, None, None] * spread - carried)


def two_steps(tracer, speeds, coeffs, wet_rows):
    rows, cols = tracer.shape[1], tracer.shape[2]
    t_r, v_r, w_r = swap([(tracer, 1, 2), (speeds, 2, 1), (wet_rows, 0, 1)], "gx")
    t_e, v_e, w_l = swap([(t_r, 2, 2), (v_r, 3, 1), (w_r, 1, 1)], "gy")
    wet_ext = jnp.broadcast_to(w_l[:, 1:2], (rows + 2, cols))
    wet_ext = jnp.concatenate([w_l[:, 0:1], wet_ext, w_l[:, 2:3]], axis=1)
    first = step(t_e, v_e, coeffs, wet_ext[None])
    a = lax.axis_index("gx")
    b = lax.axis_index("gy")
    r = jnp.arange(rows + 2)
    c = jnp.arange(cols + 2)
    row_in = ((r > 0) | (a > 0)) & ((r < rows + 1) | (a < lax.axis_size("gx") - 1))
    col_in = ((c > 0) | (b > 0)) & ((c < cols + 1) | (b < lax.axis_size("gy") - 1))
    first = jnp.where(row_in[:, None] & col_in[None, :], first, 0.0)
    return step(first, speeds, coeffs, wet_rows[None])


def exchange(exports, own_table):
    n_gx = lax.axis_size("gx")
    n_gy = lax.axis_size("gy")
    group = n_gx * n_gy
    a = lax.axis_index("gx")
    b = lax.axis_index("gy")
    shifts = jnp.arange(group, dtype=jnp.int32)
    dest = ((a + shifts // n_gy) % n_gx) * n_gy + (b + shifts % n_gy) % n_gy
    packed = exports[own_table[dest]]
    axes = ("comp", "gx", "gy")
    pieces = []
    for k in range(group):
        sa, sb = k // n_gy, k % n_gy
        perm = []
        for c in range(2):
            for i in range(n_gx):
                for j in range(n_gy):
                    src = (c * n_gx + i) * n_gy + j
                    dst = ((1 - c) * n_gx + (i + sa) % n_gx) * n_gy + (j + sb) % n_gy
                    perm.append((src, dst))
        pieces.append(lax.ppermute(packed[k], axes, perm))
    return pieces


def regrid(pieces, recv, weights, wet_rows):
    n_gx = lax.axis_size("gx")
    n_gy = lax.axis_size("gy")
    a = lax.axis_index("gx")
    b = lax.axis_index("gy")
    n_piece = len(pieces)
    cap, fld, tile = pieces[0].shape
    rows, refs = recv.shape
    source = recv // cap
    which = ((a - source // n_gy) % n_gx) * n_gy + (b - source % n_gy) % n_gy
    place = jnp.clip(recv % cap, 0, cap - 1)
    which = which.T.reshape(-1).astype(jnp.int32)
    place = place.T.reshape(-1).astype(jnp.int32)
    order = jnp.argsort(which, stable=True).astype(jnp.int32)
    counts = jnp.sum(which[None, :] == jnp.arange(n_piece, dtype=jnp.int32)[:, None], axis=1)
    bounds = jnp.concatenate([jnp.zeros((1,), jnp.int32), jnp.cumsum(counts).astype(jnp.int32)])

    def kernel(bounds_ref, order_ref, place_ref, *refs_in):
        piece_refs = refs_in[:n_piece]
        out_ref = refs_in[n_piece]
        for s in range(n_piece):
            def copy_one(j, carry, s=s):
                r = order_ref[j]
                out_ref[r // rows, r % rows] = piece_refs[s][place_ref[r]]
                return carry

            lax.fori_loop(bounds_ref[s], bounds_ref[s + 1], copy_one, 0)

    grid_spec = pltpu.PrefetchScalarGridSpec(
        num_scalar_prefetch=3,
        grid=(1,),
        in_specs=[
            pl.BlockSpec((cap, fld, tile), lambda i, c, w, q: (0, 0, 0)) for _ in range(n_piece)
        ],
        out_specs=pl.BlockSpec((refs, rows, fld, tile), lambda i, c, w, q: (0, 0, 0, 0)),
    )
    sources = pl.pallas_call(
        kernel,
        grid_spec=grid_spec,
        out_shape=jax.ShapeDtypeStruct((refs, rows, fld, tile), pieces[0].dtype),
    )(bounds, order, place, *pieces)
    summed = lax.dot_general(
        sources,
        weights,
        (((0, 3), (1, 3)), ((1,), (0,))),
        preferred_element_type=jnp.float32,
    )
    return (summed * wet_rows[:, :, None]).astype(jnp.bfloat16)


def per_device(
    state,
    velocity,
    diffusivity,
    export_proj,
    import_proj,
    intersection_weights,
    recv_slots,
    send_slots,
    land,
):
    highest = lax.Precision.HIGHEST
    section = lax.axis_index("comp")
    tracer = state[0]
    wet_tile = jnp.where(section == 0, jnp.ones(land.shape, jnp.float32), land.astype(jnp.float32))
    exports = (
        jnp.einsum("fl,lxy->xfy", export_proj[0], tracer, precision=highest) * wet_tile[:, :, None]
    ).astype(jnp.bfloat16)
    tables = send_slots[:, 0, 0]
    own_table = lax.dynamic_index_in_dim(tables, section, 0, keepdims=False)
    pieces = exchange(exports, own_table)
    imported = regrid(pieces, recv_slots[0, :, 0, :], intersection_weights[0, :, 0], wet_tile)
    wet_cells = wet_tile[None]
    tracer = two_steps(tracer, velocity[0], diffusivity[0], wet_tile)
    forcing = jnp.einsum(
        "lf,xfy->lxy", import_proj[0], imported.astype(jnp.float32), precision=highest
    )
    return ((tracer + wet_cells * forcing)[None], imported[None])


def solution(mesh):
    return jax.shard_map(
        per_device,
        mesh=mesh,
        in_specs=(
            P("comp", None, "gx", "gy"),
            P("comp", None, None, "gx", "gy"),
            P("comp", None),
            P("comp", None, None),
            P("comp", None, None),
            P("comp", "gx", "gy", None, None, None),
            P("comp", "gx", "gy", None),
            P(None, "gx", "gy", None, None),
            P("gx", "gy"),
        ),
        out_specs=(P("comp", None, "gx", "gy"), P("comp", "gx", None, "gy")),
        check_vma=False,
    )
```

```python
import jax
import jax.numpy as jnp
from jax import lax
from jax.experimental import pallas as pl
from jax.experimental.pallas import tpu as pltpu
from jax.sharding import PartitionSpec as P

STEPS = 2


def padded_2(cells, sides, width):
    for axis, dim in sides:
        count = lax.axis_size(axis)
        ends = count - 1
        head = lax.slice_in_dim(cells, 0, width, axis=dim)
        tail = lax.slice_in_dim(cells, cells.shape[dim] - width, cells.shape[dim], axis=dim)
        cells = jnp.concatenate(
            [
                lax.ppermute(tail, axis, [(i, (i + 1) % count) for i in range(ends)]),
                cells,
                lax.ppermute(head, axis, [((i + 1) % count, i) for i in range(ends)]),
            ],
            axis=dim,
        )
    return cells


def advance(tracer, speeds, coeffs, wet_mask):
    padded = padded_2(tracer.astype(jnp.bfloat16), (("gx", 1), ("gy", 2)), 1).astype(tracer.dtype)
    row_down = padded[:, 2:, 1:-1]
    row_up = padded[:, :-2, 1:-1]
    col_right = padded[:, 1:-1, 2:]
    col_left = padded[:, 1:-1, :-2]
    spread = row_down + row_up + col_right + col_left - 4.0 * tracer
    carried = 0.5 * (
        speeds[0].astype(jnp.float32) * (row_down - row_up)
        + speeds[1].astype(jnp.float32) * (col_right - col_left)
    )
    return tracer + wet_mask * (coeffs[:, None, None] * spread - carried)


def swap_pair(axis, top, bottom):
    count = lax.axis_size(axis)
    ends = count - 1
    from_prev = lax.ppermute(bottom, axis, [(i, i + 1) for i in range(ends)])
    from_next = lax.ppermute(top, axis, [(i + 1, i) for i in range(ends)])
    return from_prev, from_next


def step(ext, speeds, coeffs, wet_mask):
    centre = ext[:, 1:-1, 1:-1]
    row_down = ext[:, 2:, 1:-1]
    row_up = ext[:, :-2, 1:-1]
    col_right = ext[:, 1:-1, 2:]
    col_left = ext[:, 1:-1, :-2]
    spread = row_down + row_up + col_right + col_left - 4.0 * centre
    carried = 0.5 * (
        speeds[0].astype(jnp.float32) * (row_down - row_up)
        + speeds[1].astype(jnp.float32) * (col_right - col_left)
    )
    return centre + wet_mask * (coeffs[:, None, None] * spread - carried)


def two_steps(tracer, speeds, coeffs, wet_rows):
    lev, rows, cols = tracer.shape
    speeds = speeds.astype(jnp.float32)

    def pack_rows(t, v, w):
        return jnp.concatenate(
            [t.reshape(2 * lev, cols), v.reshape(2 * lev, cols), jnp.broadcast_to(w, (1, cols))]
        )

    prev, nxt = swap_pair(
        "gx",
        pack_rows(tracer[:, :2], speeds[:, :, :1], wet_rows[:1]),
        pack_rows(tracer[:, -2:], speeds[:, :, -1:], wet_rows[-1:]),
    )

    def rows_of(p):
        return (
            p[: 2 * lev].reshape(lev, 2, cols),
            p[2 * lev : 4 * lev].reshape(2, lev, 1, cols),
            p[4 * lev :, :1],
        )

    (tp, vp, wp), (tn, vn, wn) = rows_of(prev), rows_of(nxt)
    t_r = jnp.concatenate([tp, tracer, tn], axis=1)
    v_r = jnp.concatenate([vp, speeds, vn], axis=2)
    w_r = jnp.concatenate([wp, wet_rows, wn], axis=0)
    span = rows + 4

    def pack_cols(t, v, w):
        v = jnp.pad(v.reshape(2 * lev, rows + 2), ((0, 0), (0, 2)))
        w = jnp.pad(w.reshape(1, rows + 2), ((0, 0), (0, 2)))
        return jnp.concatenate([jnp.swapaxes(t, 1, 2).reshape(2 * lev, span), v, w])

    prev, nxt = swap_pair(
        "gy",
        pack_cols(t_r[:, :, :2], v_r[..., :1], w_r),
        pack_cols(t_r[:, :, -2:], v_r[..., -1:], w_r),
    )

    def cols_of(p):
        return (
            jnp.swapaxes(p[: 2 * lev].reshape(lev, 2, span), 1, 2),
            p[2 * lev : 4 * lev, : rows + 2].reshape(2, lev, rows + 2, 1),
            p[4 * lev :, : rows + 2].reshape(rows + 2, 1),
        )

    (tp, vp, wp), (tn, vn, wn) = cols_of(prev), cols_of(nxt)
    t_e = jnp.concatenate([tp, t_r, tn], axis=2)
    v_e = jnp.concatenate([vp, v_r, vn], axis=3)
    wet_ext = jnp.concatenate([wp, jnp.broadcast_to(w_r, (rows + 2, cols)), wn], axis=1)
    first = step(t_e, v_e, coeffs, wet_ext[None])
    a = lax.axis_index("gx")
    b = lax.axis_index("gy")
    r = jnp.arange(rows + 2)
    c = jnp.arange(cols + 2)
    row_in = ((r > 0) | (a > 0)) & ((r < rows + 1) | (a < lax.axis_size("gx") - 1))
    col_in = ((c > 0) | (b > 0)) & ((c < cols + 1) | (b < lax.axis_size("gy") - 1))
    first = jnp.where(row_in[:, None] & col_in[None, :], first, 0.0)
    return step(first, speeds, coeffs, wet_rows[None])


def exchange(exports, own_table):
    n_gx = lax.axis_size("gx")
    n_gy = lax.axis_size("gy")
    group = n_gx * n_gy
    a = lax.axis_index("gx")
    b = lax.axis_index("gy")
    shifts = jnp.arange(group, dtype=jnp.int32)
    dest = ((a + shifts // n_gy) % n_gx) * n_gy + (b + shifts % n_gy) % n_gy
    packed = exports[own_table[dest]]
    axes = ("comp", "gx", "gy")
    pieces = []
    for k in range(group):
        sa, sb = k // n_gy, k % n_gy
        perm = []
        for c in range(2):
            for i in range(n_gx):
                for j in range(n_gy):
                    src = (c * n_gx + i) * n_gy + j
                    dst = ((1 - c) * n_gx + (i + sa) % n_gx) * n_gy + (j + sb) % n_gy
                    perm.append((src, dst))
        pieces.append(lax.ppermute(packed[k], axes, perm))
    return pieces


def regrid(pieces, recv, weights, wet_rows):
    n_gx = lax.axis_size("gx")
    n_gy = lax.axis_size("gy")
    a = lax.axis_index("gx")
    b = lax.axis_index("gy")
    n_piece = len(pieces)
    cap, fld, tile = pieces[0].shape
    rows, refs = recv.shape
    source = recv // cap
    which = ((a - source // n_gy) % n_gx) * n_gy + (b - source % n_gy) % n_gy
    place = jnp.clip(recv % cap, 0, cap - 1)
    which = which.T.reshape(-1).astype(jnp.int32)
    place = place.T.reshape(-1).astype(jnp.int32)
    order = jnp.argsort(which, stable=True).astype(jnp.int32)
    counts = jnp.sum(which[None, :] == jnp.arange(n_piece, dtype=jnp.int32)[:, None], axis=1)
    bounds = jnp.concatenate([jnp.zeros((1,), jnp.int32), jnp.cumsum(counts).astype(jnp.int32)])

    def kernel(bounds_ref, order_ref, place_ref, *refs_in):
        piece_refs = refs_in[:n_piece]
        out_ref = refs_in[n_piece]
        for s in range(n_piece):
            def copy_one(j, carry, s=s):
                r = order_ref[j]
                out_ref[r // rows, r % rows] = piece_refs[s][place_ref[r]]
                return carry

            lax.fori_loop(bounds_ref[s], bounds_ref[s + 1], copy_one, 0)

    grid_spec = pltpu.PrefetchScalarGridSpec(
        num_scalar_prefetch=3,
        grid=(1,),
        in_specs=[
            pl.BlockSpec((cap, fld, tile), lambda i, c, w, q: (0, 0, 0)) for _ in range(n_piece)
        ],
        out_specs=pl.BlockSpec((refs, rows, fld, tile), lambda i, c, w, q: (0, 0, 0, 0)),
    )
    sources = pl.pallas_call(
        kernel,
        grid_spec=grid_spec,
        out_shape=jax.ShapeDtypeStruct((refs, rows, fld, tile), pieces[0].dtype),
    )(bounds, order, place, *pieces)
    summed = lax.dot_general(
        sources,
        weights,
        (((0, 3), (1, 3)), ((1,), (0,))),
        preferred_element_type=jnp.float32,
    )
    return (summed * wet_rows[:, :, None]).astype(jnp.bfloat16)


def per_device(
    state,
    velocity,
    diffusivity,
    export_proj,
    import_proj,
    intersection_weights,
    recv_slots,
    send_slots,
    land,
):
    highest = lax.Precision.HIGHEST
    section = lax.axis_index("comp")
    tracer = state[0]
    wet_tile = jnp.where(section == 0, jnp.ones(land.shape, jnp.float32), land.astype(jnp.float32))
    exports = (
        jnp.einsum("fl,lxy->xfy", export_proj[0], tracer, precision=highest) * wet_tile[:, :, None]
    ).astype(jnp.bfloat16)
    tables = send_slots[:, 0, 0]
    own_table = lax.dynamic_index_in_dim(tables, section, 0, keepdims=False)
    pieces = exchange(exports, own_table)
    imported = regrid(pieces, recv_slots[0, :, 0, :], intersection_weights[0, :, 0], wet_tile)
    wet_cells = wet_tile[None]
    tracer = two_steps(tracer, velocity[0], diffusivity[0], wet_tile)
    forcing = jnp.einsum(
        "lf,xfy->lxy", import_proj[0], imported.astype(jnp.float32), precision=highest
    )
    return ((tracer + wet_cells * forcing)[None], imported[None])


def solution(mesh):
    return jax.shard_map(
        per_device,
        mesh=mesh,
        in_specs=(
            P("comp", None, "gx", "gy"),
            P("comp", None, None, "gx", "gy"),
            P("comp", None),
            P("comp", None, None),
            P("comp", None, None),
            P("comp", "gx", "gy", None, None, None),
            P("comp", "gx", "gy", None),
            P(None, "gx", "gy", None, None),
            P("gx", "gy"),
        ),
        out_specs=(P("comp", None, "gx", "gy"), P("comp", "gx", None, "gy")),
        check_vma=False,
    )
```

```python
import jax
import jax.numpy as jnp
from jax import lax
from jax.experimental import pallas as pl
from jax.experimental.pallas import tpu as pltpu
from jax.sharding import PartitionSpec as P

STEPS = 2


def padded_2(cells, sides, width):
    for axis, dim in sides:
        count = lax.axis_size(axis)
        ends = count - 1
        head = lax.slice_in_dim(cells, 0, width, axis=dim)
        tail = lax.slice_in_dim(cells, cells.shape[dim] - width, cells.shape[dim], axis=dim)
        cells = jnp.concatenate(
            [
                lax.ppermute(tail, axis, [(i, (i + 1) % count) for i in range(ends)]),
                cells,
                lax.ppermute(head, axis, [((i + 1) % count, i) for i in range(ends)]),
            ],
            axis=dim,
        )
    return cells


def advance(tracer, speeds, coeffs, wet_mask):
    padded = padded_2(tracer.astype(jnp.bfloat16), (("gx", 1), ("gy", 2)), 1).astype(tracer.dtype)
    row_down = padded[:, 2:, 1:-1]
    row_up = padded[:, :-2, 1:-1]
    col_right = padded[:, 1:-1, 2:]
    col_left = padded[:, 1:-1, :-2]
    spread = row_down + row_up + col_right + col_left - 4.0 * tracer
    carried = 0.5 * (
        speeds[0].astype(jnp.float32) * (row_down - row_up)
        + speeds[1].astype(jnp.float32) * (col_right - col_left)
    )
    return tracer + wet_mask * (coeffs[:, None, None] * spread - carried)


def exchange(exports, own_table):
    n_gx = lax.axis_size("gx")
    n_gy = lax.axis_size("gy")
    group = n_gx * n_gy
    a = lax.axis_index("gx")
    b = lax.axis_index("gy")
    shifts = jnp.arange(group, dtype=jnp.int32)
    dest = ((a + shifts // n_gy) % n_gx) * n_gy + (b + shifts % n_gy) % n_gy
    packed = exports[own_table[dest]]
    axes = ("comp", "gx", "gy")
    pieces = []
    for k in range(group):
        sa, sb = k // n_gy, k % n_gy
        perm = []
        for c in range(2):
            for i in range(n_gx):
                for j in range(n_gy):
                    src = (c * n_gx + i) * n_gy + j
                    dst = ((1 - c) * n_gx + (i + sa) % n_gx) * n_gy + (j + sb) % n_gy
                    perm.append((src, dst))
        pieces.append(lax.ppermute(packed[k], axes, perm))
    return pieces


def regrid(pieces, recv, weights, wet_rows):
    n_gx = lax.axis_size("gx")
    n_gy = lax.axis_size("gy")
    a = lax.axis_index("gx")
    b = lax.axis_index("gy")
    n_piece = len(pieces)
    cap, fld, tile = pieces[0].shape
    rows, refs = recv.shape
    source = recv // cap
    which = ((a - source // n_gy) % n_gx) * n_gy + (b - source % n_gy) % n_gy
    place = jnp.clip(recv % cap, 0, cap - 1)
    which = which.T.reshape(-1).astype(jnp.int32)
    place = place.T.reshape(-1).astype(jnp.int32)
    order = jnp.argsort(which, stable=True).astype(jnp.int32)
    counts = jnp.sum(which[None, :] == jnp.arange(n_piece, dtype=jnp.int32)[:, None], axis=1)
    bounds = jnp.concatenate([jnp.zeros((1,), jnp.int32), jnp.cumsum(counts).astype(jnp.int32)])

    def kernel(bounds_ref, order_ref, place_ref, *refs_in):
        piece_refs = refs_in[:n_piece]
        out_ref = refs_in[n_piece]
        for s in range(n_piece):
            def copy_one(j, carry, s=s):
                r = order_ref[j]
                out_ref[r // rows, r % rows] = piece_refs[s][place_ref[r]]
                return carry

            lax.fori_loop(bounds_ref[s], bounds_ref[s + 1], copy_one, 0)

    grid_spec = pltpu.PrefetchScalarGridSpec(
        num_scalar_prefetch=3,
        grid=(1,),
        in_specs=[
            pl.BlockSpec((cap, fld, tile), lambda i, c, w, q: (0, 0, 0)) for _ in range(n_piece)
        ],
        out_specs=pl.BlockSpec((refs, rows, fld, tile), lambda i, c, w, q: (0, 0, 0, 0)),
    )
    sources = pl.pallas_call(
        kernel,
        grid_spec=grid_spec,
        out_shape=jax.ShapeDtypeStruct((refs, rows, fld, tile), pieces[0].dtype),
    )(bounds, order, place, *pieces)
    summed = lax.dot_general(
        sources,
        weights,
        (((0, 3), (1, 3)), ((1,), (0,))),
        preferred_element_type=jnp.float32,
    )
    return (summed * wet_rows[:, :, None]).astype(jnp.bfloat16)


def per_device(
    state,
    velocity,
    diffusivity,
    export_proj,
    import_proj,
    intersection_weights,
    recv_slots,
    send_slots,
    land,
):
    highest = lax.Precision.HIGHEST
    section = lax.axis_index("comp")
    tracer = state[0]
    wet_tile = jnp.where(section == 0, jnp.ones(land.shape, jnp.float32), land.astype(jnp.float32))
    exports = (
        jnp.einsum("fl,lxy->xfy", export_proj[0], tracer, precision=highest) * wet_tile[:, :, None]
    ).astype(jnp.bfloat16)
    tables = send_slots[:, 0, 0]
    own_table = lax.dynamic_index_in_dim(tables, section, 0, keepdims=False)
    pieces = exchange(exports, own_table)
    imported = regrid(pieces, recv_slots[0, :, 0, :], intersection_weights[0, :, 0], wet_tile)
    wet_cells = wet_tile[None]
    for repeat in range(STEPS):
        tracer = advance(tracer, velocity[0], diffusivity[0], wet_cells)
    proj = import_proj[0]
    hi = proj.astype(jnp.bfloat16)
    rest = proj - hi.astype(jnp.float32)
    mid = rest.astype(jnp.bfloat16)
    lo = (rest - mid.astype(jnp.float32)).astype(jnp.bfloat16)
    forcing = jnp.einsum(
        "lf,xfy->lxy",
        jnp.concatenate([hi, mid, lo], axis=1),
        jnp.concatenate([imported, imported, imported], axis=1),
        preferred_element_type=jnp.float32,
    )
    return ((tracer + wet_cells * forcing)[None], imported[None])


def solution(mesh):
    return jax.shard_map(
        per_device,
        mesh=mesh,
        in_specs=(
            P("comp", None, "gx", "gy"),
            P("comp", None, None, "gx", "gy"),
            P("comp", None),
            P("comp", None, None),
            P("comp", None, None),
            P("comp", "gx", "gy", None, None, None),
            P("comp", "gx", "gy", None),
            P(None, "gx", "gy", None, None),
            P("gx", "gy"),
        ),
        out_specs=(P("comp", None, "gx", "gy"), P("comp", "gx", None, "gy")),
        check_vma=False,
    )
```

```python
import jax
import jax.numpy as jnp
from jax import lax
from jax.experimental import pallas as pl
from jax.experimental.pallas import tpu as pltpu
from jax.sharding import PartitionSpec as P

STEPS = 2


def padded_2(cells, sides, width):
    for axis, dim in sides:
        count = lax.axis_size(axis)
        ends = count - 1
        head = lax.slice_in_dim(cells, 0, width, axis=dim)
        tail = lax.slice_in_dim(cells, cells.shape[dim] - width, cells.shape[dim], axis=dim)
        cells = jnp.concatenate(
            [
                lax.ppermute(tail, axis, [(i, (i + 1) % count) for i in range(ends)]),
                cells,
                lax.ppermute(head, axis, [((i + 1) % count, i) for i in range(ends)]),
            ],
            axis=dim,
        )
    return cells


def halo(tracer):
    return padded_2(tracer.astype(jnp.bfloat16), (("gx", 1), ("gy", 2)), 1)


def advance(tracer, speeds, coeffs, wet_mask, padded=None):
    if padded is None:
        padded = halo(tracer)
    padded = padded.astype(tracer.dtype)
    row_down = padded[:, 2:, 1:-1]
    row_up = padded[:, :-2, 1:-1]
    col_right = padded[:, 1:-1, 2:]
    col_left = padded[:, 1:-1, :-2]
    spread = row_down + row_up + col_right + col_left - 4.0 * tracer
    carried = 0.5 * (
        speeds[0].astype(jnp.float32) * (row_down - row_up)
        + speeds[1].astype(jnp.float32) * (col_right - col_left)
    )
    return tracer + wet_mask * (coeffs[:, None, None] * spread - carried)


def exchange(exports, own_table, tie):
    n_gx = lax.axis_size("gx")
    n_gy = lax.axis_size("gy")
    group = n_gx * n_gy
    a = lax.axis_index("gx")
    b = lax.axis_index("gy")
    shifts = jnp.arange(group, dtype=jnp.int32)
    dest = ((a + shifts // n_gy) % n_gx) * n_gy + (b + shifts % n_gy) % n_gy
    packed = exports[own_table[dest]]
    packed, tie = lax.optimization_barrier((packed, tie))
    axes = ("comp", "gx", "gy")
    pieces = []
    for k in range(group):
        sa, sb = k // n_gy, k % n_gy
        perm = []
        for c in range(2):
            for i in range(n_gx):
                for j in range(n_gy):
                    src = (c * n_gx + i) * n_gy + j
                    dst = ((1 - c) * n_gx + (i + sa) % n_gx) * n_gy + (j + sb) % n_gy
                    perm.append((src, dst))
        pieces.append(lax.ppermute(packed[k], axes, perm))
    return pieces, tie


def regrid(pieces, recv, weights, wet_rows):
    n_gx = lax.axis_size("gx")
    n_gy = lax.axis_size("gy")
    a = lax.axis_index("gx")
    b = lax.axis_index("gy")
    n_piece = len(pieces)
    cap, fld, tile = pieces[0].shape
    rows, refs = recv.shape
    source = recv // cap
    which = ((a - source // n_gy) % n_gx) * n_gy + (b - source % n_gy) % n_gy
    place = jnp.clip(recv % cap, 0, cap - 1)
    which = which.T.reshape(-1).astype(jnp.int32)
    place = place.T.reshape(-1).astype(jnp.int32)
    order = jnp.argsort(which, stable=True).astype(jnp.int32)
    counts = jnp.sum(which[None, :] == jnp.arange(n_piece, dtype=jnp.int32)[:, None], axis=1)
    bounds = jnp.concatenate([jnp.zeros((1,), jnp.int32), jnp.cumsum(counts).astype(jnp.int32)])

    def kernel(bounds_ref, order_ref, place_ref, *refs_in):
        piece_refs = refs_in[:n_piece]
        out_ref = refs_in[n_piece]
        for s in range(n_piece):
            def copy_one(j, carry, s=s):
                r = order_ref[j]
                out_ref[r // rows, r % rows] = piece_refs[s][place_ref[r]]
                return carry

            lax.fori_loop(bounds_ref[s], bounds_ref[s + 1], copy_one, 0)

    grid_spec = pltpu.PrefetchScalarGridSpec(
        num_scalar_prefetch=3,
        grid=(1,),
        in_specs=[
            pl.BlockSpec((cap, fld, tile), lambda i, c, w, q: (0, 0, 0)) for _ in range(n_piece)
        ],
        out_specs=pl.BlockSpec((refs, rows, fld, tile), lambda i, c, w, q: (0, 0, 0, 0)),
    )
    sources = pl.pallas_call(
        kernel,
        grid_spec=grid_spec,
        out_shape=jax.ShapeDtypeStruct((refs, rows, fld, tile), pieces[0].dtype),
    )(bounds, order, place, *pieces)
    summed = lax.dot_general(
        sources,
        weights,
        (((0, 3), (1, 3)), ((1,), (0,))),
        preferred_element_type=jnp.float32,
    )
    return (summed * wet_rows[:, :, None]).astype(jnp.bfloat16)


def per_device(
    state,
    velocity,
    diffusivity,
    export_proj,
    import_proj,
    intersection_weights,
    recv_slots,
    send_slots,
    land,
):
    highest = lax.Precision.HIGHEST
    section = lax.axis_index("comp")
    tracer = state[0]
    wet_tile = jnp.where(section == 0, jnp.ones(land.shape, jnp.float32), land.astype(jnp.float32))
    exports = (
        jnp.einsum("fl,lxy->xfy", export_proj[0], tracer, precision=highest) * wet_tile[:, :, None]
    ).astype(jnp.bfloat16)
    tables = send_slots[:, 0, 0]
    own_table = lax.dynamic_index_in_dim(tables, section, 0, keepdims=False)
    first_halo = halo(tracer)
    pieces, first_halo = exchange(exports, own_table, first_halo)
    imported = regrid(pieces, recv_slots[0, :, 0, :], intersection_weights[0, :, 0], wet_tile)
    wet_cells = wet_tile[None]
    for repeat in range(STEPS):
        tracer = advance(
            tracer, velocity[0], diffusivity[0], wet_cells, first_halo if repeat == 0 else None
        )
    forcing = jnp.einsum(
        "lf,xfy->lxy", import_proj[0], imported.astype(jnp.float32), precision=highest
    )
    return ((tracer + wet_cells * forcing)[None], imported[None])


def solution(mesh):
    return jax.shard_map(
        per_device,
        mesh=mesh,
        in_specs=(
            P("comp", None, "gx", "gy"),
            P("comp", None, None, "gx", "gy"),
            P("comp", None),
            P("comp", None, None),
            P("comp", None, None),
            P("comp", "gx", "gy", None, None, None),
            P("comp", "gx", "gy", None),
            P(None, "gx", "gy", None, None),
            P("gx", "gy"),
        ),
        out_specs=(P("comp", None, "gx", "gy"), P("comp", "gx", None, "gy")),
        check_vma=False,
    )
```

```python
import jax
import jax.numpy as jnp
from jax import lax
from jax.experimental import pallas as pl
from jax.experimental.pallas import tpu as pltpu
from jax.sharding import PartitionSpec as P

STEPS = 2


def padded_2(cells, sides, width):
    for axis, dim in sides:
        count = lax.axis_size(axis)
        ends = count - 1
        head = lax.slice_in_dim(cells, 0, width, axis=dim)
        tail = lax.slice_in_dim(cells, cells.shape[dim] - width, cells.shape[dim], axis=dim)
        cells = jnp.concatenate(
            [
                lax.ppermute(tail, axis, [(i, (i + 1) % count) for i in range(ends)]),
                cells,
                lax.ppermute(head, axis, [((i + 1) % count, i) for i in range(ends)]),
            ],
            axis=dim,
        )
    return cells


def advance(tracer, speeds, coeffs, wet_mask):
    padded = padded_2(tracer, (("gx", 1), ("gy", 2)), 1)
    row_down = padded[:, 2:, 1:-1]
    row_up = padded[:, :-2, 1:-1]
    col_right = padded[:, 1:-1, 2:]
    col_left = padded[:, 1:-1, :-2]
    spread = row_down + row_up + col_right + col_left - 4.0 * tracer
    carried = 0.5 * (
        speeds[0].astype(jnp.float32) * (row_down - row_up)
        + speeds[1].astype(jnp.float32) * (col_right - col_left)
    )
    return tracer + wet_mask * (coeffs[:, None, None] * spread - carried)


def exchange(exports, own_table):
    n_gx = lax.axis_size("gx")
    n_gy = lax.axis_size("gy")
    group = n_gx * n_gy
    a = lax.axis_index("gx")
    b = lax.axis_index("gy")
    shifts = jnp.arange(group, dtype=jnp.int32)
    dest = ((a + shifts // n_gy) % n_gx) * n_gy + (b + shifts % n_gy) % n_gy
    packed = exports[own_table[dest]]
    axes = ("comp", "gx", "gy")
    pieces = []
    for k in range(group):
        sa, sb = k // n_gy, k % n_gy
        perm = []
        for c in range(2):
            for i in range(n_gx):
                for j in range(n_gy):
                    src = (c * n_gx + i) * n_gy + j
                    dst = ((1 - c) * n_gx + (i + sa) % n_gx) * n_gy + (j + sb) % n_gy
                    perm.append((src, dst))
        pieces.append(lax.ppermute(packed[k], axes, perm))
    return pieces


def regrid(pieces, recv, weights, wet_rows):
    n_gx = lax.axis_size("gx")
    n_gy = lax.axis_size("gy")
    a = lax.axis_index("gx")
    b = lax.axis_index("gy")
    n_piece = len(pieces)
    cap, fld, tile = pieces[0].shape
    rows, refs = recv.shape
    source = recv // cap
    which = ((a - source // n_gy) % n_gx) * n_gy + (b - source % n_gy) % n_gy
    place = jnp.clip(recv % cap, 0, cap - 1)
    which = which.T.reshape(-1).astype(jnp.int32)
    place = place.T.reshape(-1).astype(jnp.int32)
    order = jnp.argsort(which, stable=True).astype(jnp.int32)
    counts = jnp.sum(which[None, :] == jnp.arange(n_piece, dtype=jnp.int32)[:, None], axis=1)
    bounds = jnp.concatenate([jnp.zeros((1,), jnp.int32), jnp.cumsum(counts).astype(jnp.int32)])

    def kernel(bounds_ref, order_ref, place_ref, *refs_in):
        piece_refs = refs_in[:n_piece]
        out_ref = refs_in[n_piece]
        for s in range(n_piece):
            def copy_one(j, carry, s=s):
                r = order_ref[j]
                out_ref[r // rows, r % rows] = piece_refs[s][place_ref[r]]
                return carry

            lax.fori_loop(bounds_ref[s], bounds_ref[s + 1], copy_one, 0)

    grid_spec = pltpu.PrefetchScalarGridSpec(
        num_scalar_prefetch=3,
        grid=(1,),
        in_specs=[
            pl.BlockSpec((cap, fld, tile), lambda i, c, w, q: (0, 0, 0)) for _ in range(n_piece)
        ],
        out_specs=pl.BlockSpec((refs, rows, fld, tile), lambda i, c, w, q: (0, 0, 0, 0)),
    )
    sources = pl.pallas_call(
        kernel,
        grid_spec=grid_spec,
        out_shape=jax.ShapeDtypeStruct((refs, rows, fld, tile), pieces[0].dtype),
    )(bounds, order, place, *pieces)
    summed = lax.dot_general(
        sources,
        weights,
        (((0, 3), (1, 3)), ((1,), (0,))),
        preferred_element_type=jnp.float32,
    )
    return (summed * wet_rows[:, :, None]).astype(jnp.bfloat16)


def per_device(
    state,
    velocity,
    diffusivity,
    export_proj,
    import_proj,
    intersection_weights,
    recv_slots,
    send_slots,
    land,
):
    highest = lax.Precision.HIGHEST
    section = lax.axis_index("comp")
    tracer = state[0]
    wet_tile = jnp.where(section == 0, jnp.ones(land.shape, jnp.float32), land.astype(jnp.float32))
    exports = (
        jnp.einsum("fl,lxy->xfy", export_proj[0], tracer, precision=highest) * wet_tile[:, :, None]
    ).astype(jnp.bfloat16)
    tables = send_slots[:, 0, 0]
    own_table = lax.dynamic_index_in_dim(tables, section, 0, keepdims=False)
    pieces = exchange(exports, own_table)
    imported = regrid(pieces, recv_slots[0, :, 0, :], intersection_weights[0, :, 0], wet_tile)
    wet_cells = wet_tile[None]
    for repeat in range(STEPS):
        tracer = advance(tracer, velocity[0], diffusivity[0], wet_cells)
    forcing = jnp.einsum(
        "lf,xfy->lxy", import_proj[0], imported.astype(jnp.float32), precision=highest
    )
    return ((tracer + wet_cells * forcing)[None], imported[None])


def solution(mesh):
    return jax.shard_map(
        per_device,
        mesh=mesh,
        in_specs=(
            P("comp", None, "gx", "gy"),
            P("comp", None, None, "gx", "gy"),
            P("comp", None),
            P("comp", None, None),
            P("comp", None, None),
            P("comp", "gx", "gy", None, None, None),
            P("comp", "gx", "gy", None),
            P(None, "gx", "gy", None, None),
            P("gx", "gy"),
        ),
        out_specs=(P("comp", None, "gx", "gy"), P("comp", "gx", None, "gy")),
        check_vma=False,
    )
```

```python
import jax
import jax.numpy as jnp
from jax import lax
from jax.experimental import pallas as pl
from jax.experimental.pallas import tpu as pltpu
from jax.sharding import PartitionSpec as P

STEPS = 2


def padded_2(cells, sides, width):
    for axis, dim in sides:
        count = lax.axis_size(axis)
        ends = count - 1
        head = lax.slice_in_dim(cells, 0, width, axis=dim)
        tail = lax.slice_in_dim(cells, cells.shape[dim] - width, cells.shape[dim], axis=dim)
        cells = jnp.concatenate(
            [
                lax.ppermute(tail, axis, [(i, (i + 1) % count) for i in range(ends)]),
                cells,
                lax.ppermute(head, axis, [((i + 1) % count, i) for i in range(ends)]),
            ],
            axis=dim,
        )
    return cells


def advance(tracer, speeds, coeffs, wet_mask):
    padded = padded_2(tracer, (("gx", 1), ("gy", 2)), 1)
    row_down = padded[:, 2:, 1:-1]
    row_up = padded[:, :-2, 1:-1]
    col_right = padded[:, 1:-1, 2:]
    col_left = padded[:, 1:-1, :-2]
    spread = row_down + row_up + col_right + col_left - 4.0 * tracer
    carried = 0.5 * (
        speeds[0].astype(jnp.float32) * (row_down - row_up)
        + speeds[1].astype(jnp.float32) * (col_right - col_left)
    )
    return tracer + wet_mask * (coeffs[:, None, None] * spread - carried)


def exchange(exports, own_table):
    n_gx = lax.axis_size("gx")
    n_gy = lax.axis_size("gy")
    group = n_gx * n_gy
    a = lax.axis_index("gx")
    b = lax.axis_index("gy")
    shifts = jnp.arange(group, dtype=jnp.int32)
    dest = ((a + shifts // n_gy) % n_gx) * n_gy + (b + shifts % n_gy) % n_gy
    packed = exports[own_table[dest]]
    axes = ("comp", "gx", "gy")
    pieces = []
    for k in range(group):
        sa, sb = k // n_gy, k % n_gy
        perm = []
        for c in range(2):
            for i in range(n_gx):
                for j in range(n_gy):
                    src = (c * n_gx + i) * n_gy + j
                    dst = ((1 - c) * n_gx + (i + sa) % n_gx) * n_gy + (j + sb) % n_gy
                    perm.append((src, dst))
        pieces.append(lax.ppermute(packed[k], axes, perm))
    return pieces


def regrid(pieces, recv, weights, wet_rows):
    n_gx = lax.axis_size("gx")
    n_gy = lax.axis_size("gy")
    a = lax.axis_index("gx")
    b = lax.axis_index("gy")
    n_piece = len(pieces)
    cap, fld, tile = pieces[0].shape
    rows, refs = recv.shape
    source = recv // cap
    which = ((a - source // n_gy) % n_gx) * n_gy + (b - source % n_gy) % n_gy
    place = jnp.clip(recv % cap, 0, cap - 1)
    which = which.T.reshape(-1).astype(jnp.int32)
    place = place.T.reshape(-1).astype(jnp.int32)
    count = which.shape[0]
    order = lax.sort(which * count + jnp.arange(count, dtype=jnp.int32)) % count
    counts = jnp.sum(which[None, :] == jnp.arange(n_piece, dtype=jnp.int32)[:, None], axis=1)
    bounds = jnp.concatenate([jnp.zeros((1,), jnp.int32), jnp.cumsum(counts).astype(jnp.int32)])

    def kernel(bounds_ref, order_ref, place_ref, *refs_in):
        piece_refs = refs_in[:n_piece]
        out_ref = refs_in[n_piece]
        for s in range(n_piece):
            def copy_one(j, carry, s=s):
                r = order_ref[j]
                out_ref[r // rows, r % rows] = piece_refs[s][place_ref[r]]
                return carry

            lax.fori_loop(bounds_ref[s], bounds_ref[s + 1], copy_one, 0)

    grid_spec = pltpu.PrefetchScalarGridSpec(
        num_scalar_prefetch=3,
        grid=(1,),
        in_specs=[
            pl.BlockSpec((cap, fld, tile), lambda i, c, w, q: (0, 0, 0)) for _ in range(n_piece)
        ],
        out_specs=pl.BlockSpec((refs, rows, fld, tile), lambda i, c, w, q: (0, 0, 0, 0)),
    )
    sources = pl.pallas_call(
        kernel,
        grid_spec=grid_spec,
        out_shape=jax.ShapeDtypeStruct((refs, rows, fld, tile), pieces[0].dtype),
    )(bounds, order, place, *pieces)
    summed = lax.dot_general(
        sources,
        weights,
        (((0, 3), (1, 3)), ((1,), (0,))),
        preferred_element_type=jnp.float32,
    )
    return (summed * wet_rows[:, :, None]).astype(jnp.bfloat16)


def per_device(
    state,
    velocity,
    diffusivity,
    export_proj,
    import_proj,
    intersection_weights,
    recv_slots,
    send_slots,
    land,
):
    highest = lax.Precision.HIGHEST
    section = lax.axis_index("comp")
    tracer = state[0]
    wet_tile = jnp.where(section == 0, jnp.ones(land.shape, jnp.float32), land.astype(jnp.float32))
    exports = (
        jnp.einsum("fl,lxy->xfy", export_proj[0], tracer, precision=highest) * wet_tile[:, :, None]
    ).astype(jnp.bfloat16)
    tables = send_slots[:, 0, 0]
    own_table = lax.dynamic_index_in_dim(tables, section, 0, keepdims=False)
    pieces = exchange(exports, own_table)
    imported = regrid(pieces, recv_slots[0, :, 0, :], intersection_weights[0, :, 0], wet_tile)
    wet_cells = wet_tile[None]
    for repeat in range(STEPS):
        tracer = advance(tracer, velocity[0], diffusivity[0], wet_cells)
    forcing = jnp.einsum(
        "lf,xfy->lxy", import_proj[0], imported.astype(jnp.float32), precision=highest
    )
    return ((tracer + wet_cells * forcing)[None], imported[None])


def solution(mesh):
    return jax.shard_map(
        per_device,
        mesh=mesh,
        in_specs=(
            P("comp", None, "gx", "gy"),
            P("comp", None, None, "gx", "gy"),
            P("comp", None),
            P("comp", None, None),
            P("comp", None, None),
            P("comp", "gx", "gy", None, None, None),
            P("comp", "gx", "gy", None),
            P(None, "gx", "gy", None, None),
            P("gx", "gy"),
        ),
        out_specs=(P("comp", None, "gx", "gy"), P("comp", "gx", None, "gy")),
        check_vma=False,
    )
```

```python
import jax
import jax.numpy as jnp
from jax import lax
from jax.experimental import pallas as pl
from jax.experimental.pallas import tpu as pltpu
from jax.sharding import PartitionSpec as P

STEPS = 2


def padded_2(cells, sides, width):
    for axis, dim in sides:
        count = lax.axis_size(axis)
        ends = count - 1
        head = lax.slice_in_dim(cells, 0, width, axis=dim)
        tail = lax.slice_in_dim(cells, cells.shape[dim] - width, cells.shape[dim], axis=dim)
        cells = jnp.concatenate(
            [
                lax.ppermute(tail, axis, [(i, (i + 1) % count) for i in range(ends)]),
                cells,
                lax.ppermute(head, axis, [((i + 1) % count, i) for i in range(ends)]),
            ],
            axis=dim,
        )
    return cells


def advance(tracer, speeds, coeffs, wet_mask):
    padded = padded_2(tracer, (("gx", 1), ("gy", 2)), 1)
    row_down = padded[:, 2:, 1:-1]
    row_up = padded[:, :-2, 1:-1]
    col_right = padded[:, 1:-1, 2:]
    col_left = padded[:, 1:-1, :-2]
    spread = row_down + row_up + col_right + col_left - 4.0 * tracer
    carried = 0.5 * (
        speeds[0].astype(jnp.float32) * (row_down - row_up)
        + speeds[1].astype(jnp.float32) * (col_right - col_left)
    )
    return tracer + wet_mask * (coeffs[:, None, None] * spread - carried)


def exchange(exports, own_table):
    n_gx = lax.axis_size("gx")
    n_gy = lax.axis_size("gy")
    group = n_gx * n_gy
    a = lax.axis_index("gx")
    b = lax.axis_index("gy")
    shifts = jnp.arange(group, dtype=jnp.int32)
    dest = ((a + shifts // n_gy) % n_gx) * n_gy + (b + shifts % n_gy) % n_gy
    packed = exports[own_table[dest]]
    axes = ("comp", "gx", "gy")
    pieces = []
    for k in range(group):
        sa, sb = k // n_gy, k % n_gy
        perm = []
        for c in range(2):
            for i in range(n_gx):
                for j in range(n_gy):
                    src = (c * n_gx + i) * n_gy + j
                    dst = ((1 - c) * n_gx + (i + sa) % n_gx) * n_gy + (j + sb) % n_gy
                    perm.append((src, dst))
        pieces.append(lax.ppermute(packed[k], axes, perm))
    return pieces


def regrid(pieces, recv, weights, wet_rows):
    n_gx = lax.axis_size("gx")
    n_gy = lax.axis_size("gy")
    a = lax.axis_index("gx")
    b = lax.axis_index("gy")
    n_piece = len(pieces)
    cap, fld, tile = pieces[0].shape
    rows, refs = recv.shape
    source = recv // cap
    which = ((a - source // n_gy) % n_gx) * n_gy + (b - source % n_gy) % n_gy
    place = jnp.clip(recv % cap, 0, cap - 1)
    which = which.T.reshape(-1).astype(jnp.int32)
    place = place.T.reshape(-1).astype(jnp.int32)
    count = which.shape[0]
    order = lax.sort(which * count + jnp.arange(count, dtype=jnp.int32)) % count
    counts = jnp.sum(which[None, :] == jnp.arange(n_piece, dtype=jnp.int32)[:, None], axis=1)
    bounds = jnp.concatenate([jnp.zeros((1,), jnp.int32), jnp.cumsum(counts).astype(jnp.int32)])

    def kernel(bounds_ref, order_ref, place_ref, *refs_in):
        piece_refs = refs_in[:n_piece]
        out_ref = refs_in[n_piece]
        for s in range(n_piece):
            def copy_one(j, s=s):
                r = order_ref[j]
                out_ref[r // rows, r % rows] = piece_refs[s][place_ref[r]]

            lo = bounds_ref[s]
            hi = bounds_ref[s + 1]
            quads = (hi - lo) // 4

            def copy_four(j, carry, lo=lo, copy_one=copy_one):
                for u in range(4):
                    copy_one(lo + 4 * j + u)
                return carry

            def copy_tail(j, carry, copy_one=copy_one):
                copy_one(j)
                return carry

            lax.fori_loop(0, quads, copy_four, 0)
            lax.fori_loop(lo + 4 * quads, hi, copy_tail, 0)

    grid_spec = pltpu.PrefetchScalarGridSpec(
        num_scalar_prefetch=3,
        grid=(1,),
        in_specs=[
            pl.BlockSpec((cap, fld, tile), lambda i, c, w, q: (0, 0, 0)) for _ in range(n_piece)
        ],
        out_specs=pl.BlockSpec((refs, rows, fld, tile), lambda i, c, w, q: (0, 0, 0, 0)),
    )
    sources = pl.pallas_call(
        kernel,
        grid_spec=grid_spec,
        out_shape=jax.ShapeDtypeStruct((refs, rows, fld, tile), pieces[0].dtype),
    )(bounds, order, place, *pieces)
    summed = lax.dot_general(
        sources,
        weights,
        (((0, 3), (1, 3)), ((1,), (0,))),
        preferred_element_type=jnp.float32,
    )
    return (summed * wet_rows[:, :, None]).astype(jnp.bfloat16)


def per_device(
    state,
    velocity,
    diffusivity,
    export_proj,
    import_proj,
    intersection_weights,
    recv_slots,
    send_slots,
    land,
):
    highest = lax.Precision.HIGHEST
    section = lax.axis_index("comp")
    tracer = state[0]
    wet_tile = jnp.where(section == 0, jnp.ones(land.shape, jnp.float32), land.astype(jnp.float32))
    exports = (
        jnp.einsum("fl,lxy->xfy", export_proj[0], tracer, precision=highest) * wet_tile[:, :, None]
    ).astype(jnp.bfloat16)
    tables = send_slots[:, 0, 0]
    own_table = lax.dynamic_index_in_dim(tables, section, 0, keepdims=False)
    pieces = exchange(exports, own_table)
    imported = regrid(pieces, recv_slots[0, :, 0, :], intersection_weights[0, :, 0], wet_tile)
    wet_cells = wet_tile[None]
    for repeat in range(STEPS):
        tracer = advance(tracer, velocity[0], diffusivity[0], wet_cells)
    forcing = jnp.einsum(
        "lf,xfy->lxy", import_proj[0], imported.astype(jnp.float32), precision=highest
    )
    return ((tracer + wet_cells * forcing)[None], imported[None])


def solution(mesh):
    return jax.shard_map(
        per_device,
        mesh=mesh,
        in_specs=(
            P("comp", None, "gx", "gy"),
            P("comp", None, None, "gx", "gy"),
            P("comp", None),
            P("comp", None, None),
            P("comp", None, None),
            P("comp", "gx", "gy", None, None, None),
            P("comp", "gx", "gy", None),
            P(None, "gx", "gy", None, None),
            P("gx", "gy"),
        ),
        out_specs=(P("comp", None, "gx", "gy"), P("comp", "gx", None, "gy")),
        check_vma=False,
    )
```

```python
import jax
import jax.numpy as jnp
from jax import lax
from jax.experimental import pallas as pl
from jax.experimental.pallas import tpu as pltpu
from jax.sharding import PartitionSpec as P

STEPS = 2


def padded_2(cells, sides, width):
    for axis, dim in sides:
        count = lax.axis_size(axis)
        ends = count - 1
        head = lax.slice_in_dim(cells, 0, width, axis=dim)
        tail = lax.slice_in_dim(cells, cells.shape[dim] - width, cells.shape[dim], axis=dim)
        cells = jnp.concatenate(
            [
                lax.ppermute(tail, axis, [(i, (i + 1) % count) for i in range(ends)]),
                cells,
                lax.ppermute(head, axis, [((i + 1) % count, i) for i in range(ends)]),
            ],
            axis=dim,
        )
    return cells


def advance(tracer, speeds, coeffs, wet_mask):
    padded = padded_2(tracer, (("gx", 1), ("gy", 2)), 1)
    row_down = padded[:, 2:, 1:-1]
    row_up = padded[:, :-2, 1:-1]
    col_right = padded[:, 1:-1, 2:]
    col_left = padded[:, 1:-1, :-2]
    spread = row_down + row_up + col_right + col_left - 4.0 * tracer
    carried = 0.5 * (
        speeds[0].astype(jnp.float32) * (row_down - row_up)
        + speeds[1].astype(jnp.float32) * (col_right - col_left)
    )
    return tracer + wet_mask * (coeffs[:, None, None] * spread - carried)


def exchange(exports, own_table):
    n_gx = lax.axis_size("gx")
    n_gy = lax.axis_size("gy")
    group = n_gx * n_gy
    a = lax.axis_index("gx")
    b = lax.axis_index("gy")
    shifts = jnp.arange(group, dtype=jnp.int32)
    dest = ((a + shifts // n_gy) % n_gx) * n_gy + (b + shifts % n_gy) % n_gy
    packed = exports[own_table[dest]]
    axes = ("comp", "gx", "gy")
    pieces = []
    for k in range(group):
        sa, sb = k // n_gy, k % n_gy
        perm = []
        for c in range(2):
            for i in range(n_gx):
                for j in range(n_gy):
                    src = (c * n_gx + i) * n_gy + j
                    dst = ((1 - c) * n_gx + (i + sa) % n_gx) * n_gy + (j + sb) % n_gy
                    perm.append((src, dst))
        pieces.append(lax.ppermute(packed[k], axes, perm))
    return pieces


def regrid(pieces, recv, weights, wet_rows):
    n_gx = lax.axis_size("gx")
    n_gy = lax.axis_size("gy")
    a = lax.axis_index("gx")
    b = lax.axis_index("gy")
    n_piece = len(pieces)
    cap, fld, tile = pieces[0].shape
    rows, refs = recv.shape
    source = recv // cap
    which = ((a - source // n_gy) % n_gx) * n_gy + (b - source % n_gy) % n_gy
    place = jnp.clip(recv % cap, 0, cap - 1)
    which = which.T.reshape(-1).astype(jnp.int32)
    place = place.T.reshape(-1).astype(jnp.int32)
    count = which.shape[0]
    order = lax.sort(which * count + jnp.arange(count, dtype=jnp.int32)) % count
    counts = jnp.sum(which[None, :] == jnp.arange(n_piece, dtype=jnp.int32)[:, None], axis=1)
    bounds = jnp.concatenate([jnp.zeros((1,), jnp.int32), jnp.cumsum(counts).astype(jnp.int32)])

    def kernel(bounds_ref, order_ref, place_ref, *refs_in):
        piece_refs = refs_in[:n_piece]
        out_ref = refs_in[n_piece]
        for s in range(n_piece):
            def copy_one(j, s=s):
                r = order_ref[j]
                out_ref[r // rows, r % rows] = piece_refs[s][place_ref[r]]

            lo = bounds_ref[s]
            hi = bounds_ref[s + 1]
            quads = (hi - lo) // 8

            def copy_four(j, carry, lo=lo, copy_one=copy_one):
                for u in range(8):
                    copy_one(lo + 8 * j + u)
                return carry

            def copy_tail(j, carry, copy_one=copy_one):
                copy_one(j)
                return carry

            lax.fori_loop(0, quads, copy_four, 0)
            lax.fori_loop(lo + 8 * quads, hi, copy_tail, 0)

    grid_spec = pltpu.PrefetchScalarGridSpec(
        num_scalar_prefetch=3,
        grid=(1,),
        in_specs=[
            pl.BlockSpec((cap, fld, tile), lambda i, c, w, q: (0, 0, 0)) for _ in range(n_piece)
        ],
        out_specs=pl.BlockSpec((refs, rows, fld, tile), lambda i, c, w, q: (0, 0, 0, 0)),
    )
    sources = pl.pallas_call(
        kernel,
        grid_spec=grid_spec,
        out_shape=jax.ShapeDtypeStruct((refs, rows, fld, tile), pieces[0].dtype),
    )(bounds, order, place, *pieces)
    summed = lax.dot_general(
        sources,
        weights,
        (((0, 3), (1, 3)), ((1,), (0,))),
        preferred_element_type=jnp.float32,
    )
    return (summed * wet_rows[:, :, None]).astype(jnp.bfloat16)


def per_device(
    state,
    velocity,
    diffusivity,
    export_proj,
    import_proj,
    intersection_weights,
    recv_slots,
    send_slots,
    land,
):
    highest = lax.Precision.HIGHEST
    section = lax.axis_index("comp")
    tracer = state[0]
    wet_tile = jnp.where(section == 0, jnp.ones(land.shape, jnp.float32), land.astype(jnp.float32))
    exports = (
        jnp.einsum("fl,lxy->xfy", export_proj[0], tracer, precision=highest) * wet_tile[:, :, None]
    ).astype(jnp.bfloat16)
    tables = send_slots[:, 0, 0]
    own_table = lax.dynamic_index_in_dim(tables, section, 0, keepdims=False)
    pieces = exchange(exports, own_table)
    imported = regrid(pieces, recv_slots[0, :, 0, :], intersection_weights[0, :, 0], wet_tile)
    wet_cells = wet_tile[None]
    for repeat in range(STEPS):
        tracer = advance(tracer, velocity[0], diffusivity[0], wet_cells)
    forcing = jnp.einsum(
        "lf,xfy->lxy", import_proj[0], imported.astype(jnp.float32), precision=highest
    )
    return ((tracer + wet_cells * forcing)[None], imported[None])


def solution(mesh):
    return jax.shard_map(
        per_device,
        mesh=mesh,
        in_specs=(
            P("comp", None, "gx", "gy"),
            P("comp", None, None, "gx", "gy"),
            P("comp", None),
            P("comp", None, None),
            P("comp", None, None),
            P("comp", "gx", "gy", None, None, None),
            P("comp", "gx", "gy", None),
            P(None, "gx", "gy", None, None),
            P("gx", "gy"),
        ),
        out_specs=(P("comp", None, "gx", "gy"), P("comp", "gx", None, "gy")),
        check_vma=False,
    )
```

```python
import jax
import jax.numpy as jnp
from jax import lax
from jax.experimental import pallas as pl
from jax.experimental.pallas import tpu as pltpu
from jax.sharding import PartitionSpec as P

STEPS = 2


def padded_2(cells, sides, width):
    for axis, dim in sides:
        count = lax.axis_size(axis)
        ends = count - 1
        head = lax.slice_in_dim(cells, 0, width, axis=dim)
        tail = lax.slice_in_dim(cells, cells.shape[dim] - width, cells.shape[dim], axis=dim)
        cells = jnp.concatenate(
            [
                lax.ppermute(tail, axis, [(i, (i + 1) % count) for i in range(ends)]),
                cells,
                lax.ppermute(head, axis, [((i + 1) % count, i) for i in range(ends)]),
            ],
            axis=dim,
        )
    return cells


def advance(tracer, speeds, coeffs, wet_mask):
    padded = padded_2(tracer, (("gx", 1), ("gy", 2)), 1)
    row_down = padded[:, 2:, 1:-1]
    row_up = padded[:, :-2, 1:-1]
    col_right = padded[:, 1:-1, 2:]
    col_left = padded[:, 1:-1, :-2]
    spread = row_down + row_up + col_right + col_left - 4.0 * tracer
    carried = 0.5 * (
        speeds[0].astype(jnp.float32) * (row_down - row_up)
        + speeds[1].astype(jnp.float32) * (col_right - col_left)
    )
    return tracer + wet_mask * (coeffs[:, None, None] * spread - carried)


def exchange(exports, own_table):
    n_gx = lax.axis_size("gx")
    n_gy = lax.axis_size("gy")
    group = n_gx * n_gy
    a = lax.axis_index("gx")
    b = lax.axis_index("gy")
    shifts = jnp.arange(group, dtype=jnp.int32)
    dest = ((a + shifts // n_gy) % n_gx) * n_gy + (b + shifts % n_gy) % n_gy
    packed = exports[own_table[dest]]
    axes = ("comp", "gx", "gy")
    pieces = []
    for k in range(group):
        sa, sb = k // n_gy, k % n_gy
        perm = []
        for c in range(2):
            for i in range(n_gx):
                for j in range(n_gy):
                    src = (c * n_gx + i) * n_gy + j
                    dst = ((1 - c) * n_gx + (i + sa) % n_gx) * n_gy + (j + sb) % n_gy
                    perm.append((src, dst))
        pieces.append(lax.ppermute(packed[k], axes, perm))
    return pieces


def regrid(pieces, recv, weights, wet_rows):
    n_gx = lax.axis_size("gx")
    n_gy = lax.axis_size("gy")
    a = lax.axis_index("gx")
    b = lax.axis_index("gy")
    n_piece = len(pieces)
    cap, fld, tile = pieces[0].shape
    rows, refs = recv.shape
    source = recv // cap
    which = ((a - source // n_gy) % n_gx) * n_gy + (b - source % n_gy) % n_gy
    place = jnp.clip(recv % cap, 0, cap - 1)
    which = which.T.reshape(-1).astype(jnp.int32)
    place = place.T.reshape(-1).astype(jnp.int32)
    count = which.shape[0]
    order = lax.sort(which * count + jnp.arange(count, dtype=jnp.int32)) % count
    counts = jnp.sum(which[None, :] == jnp.arange(n_piece, dtype=jnp.int32)[:, None], axis=1)
    bounds = jnp.concatenate([jnp.zeros((1,), jnp.int32), jnp.cumsum(counts).astype(jnp.int32)])

    def kernel(bounds_ref, order_ref, place_ref, *refs_in):
        piece_refs = refs_in[:n_piece]
        out_ref = refs_in[n_piece]
        for s in range(n_piece):
            def copy_one(j, s=s):
                r = order_ref[j]
                out_ref[r // rows, r % rows] = piece_refs[s][place_ref[r]]

            lo = bounds_ref[s]
            hi = bounds_ref[s + 1]
            quads = (hi - lo) // 4

            def copy_four(j, carry, lo=lo, copy_one=copy_one):
                for u in range(4):
                    copy_one(lo + 4 * j + u)
                return carry

            def copy_tail(j, carry, copy_one=copy_one):
                copy_one(j)
                return carry

            lax.fori_loop(0, quads, copy_four, 0)
            lax.fori_loop(lo + 4 * quads, hi, copy_tail, 0)

    grid_spec = pltpu.PrefetchScalarGridSpec(
        num_scalar_prefetch=3,
        grid=(1,),
        in_specs=[
            pl.BlockSpec((cap, fld, tile), lambda i, c, w, q: (0, 0, 0)) for _ in range(n_piece)
        ],
        out_specs=pl.BlockSpec((refs, rows, fld, tile), lambda i, c, w, q: (0, 0, 0, 0)),
    )
    sources = pl.pallas_call(
        kernel,
        grid_spec=grid_spec,
        out_shape=jax.ShapeDtypeStruct((refs, rows, fld, tile), pieces[0].dtype),
    )(bounds, order, place, *pieces)
    summed = lax.dot_general(
        sources,
        weights,
        (((0, 3), (1, 3)), ((1,), (0,))),
        preferred_element_type=jnp.float32,
    )
    return (summed * wet_rows[:, :, None]).astype(jnp.bfloat16)


def per_device(
    state,
    velocity,
    diffusivity,
    export_proj,
    import_proj,
    intersection_weights,
    recv_slots,
    send_slots,
    land,
):
    highest = lax.Precision.HIGHEST
    section = lax.axis_index("comp")
    tracer = state[0]
    wet_tile = jnp.where(section == 0, jnp.ones(land.shape, jnp.float32), land.astype(jnp.float32))
    exports = (
        jnp.einsum("fl,lxy->xfy", export_proj[0], tracer, precision=lax.Precision.HIGH)
        * wet_tile[:, :, None]
    ).astype(jnp.bfloat16)
    tables = send_slots[:, 0, 0]
    own_table = lax.dynamic_index_in_dim(tables, section, 0, keepdims=False)
    pieces = exchange(exports, own_table)
    imported = regrid(pieces, recv_slots[0, :, 0, :], intersection_weights[0, :, 0], wet_tile)
    wet_cells = wet_tile[None]
    for repeat in range(STEPS):
        tracer = advance(tracer, velocity[0], diffusivity[0], wet_cells)
    forcing = jnp.einsum(
        "lf,xfy->lxy", import_proj[0], imported.astype(jnp.float32), precision=highest
    )
    return ((tracer + wet_cells * forcing)[None], imported[None])


def solution(mesh):
    return jax.shard_map(
        per_device,
        mesh=mesh,
        in_specs=(
            P("comp", None, "gx", "gy"),
            P("comp", None, None, "gx", "gy"),
            P("comp", None),
            P("comp", None, None),
            P("comp", None, None),
            P("comp", "gx", "gy", None, None, None),
            P("comp", "gx", "gy", None),
            P(None, "gx", "gy", None, None),
            P("gx", "gy"),
        ),
        out_specs=(P("comp", None, "gx", "gy"), P("comp", "gx", None, "gy")),
        check_vma=False,
    )
```
